128 devices in a mesh: tm: 16 (over z, y_lo, core), freq: 8 (over y_hi, x).
Axes of the slice: x: 4, y: 4 (y_hi: 2, y_lo: 2; y = y_hi * 2 + y_lo), z: 4, core: 2. Of those that a mesh axis runs over, the one named last changes fastest.
Arguments:
- tokens: bfloat16 [256, 128, 1024], P('tm', 'freq'), may hold values from -16 to 16
- w_query: bfloat16 [1024, 1024], replicated, may hold values from -1 to 1
- w_key: bfloat16 [1024, 1024], replicated, may hold values from -1 to 1
- w_value: bfloat16 [1024, 1024], replicated, may hold values from -0.1875 to 0.1875
- w_out: bfloat16 [1024, 1024], replicated, may hold values from -0.75 to 0.75
- d_out: bfloat16 [256, 128, 1024], P('tm', 'freq'), may hold values from -6 to 6
Outputs:
- output: bfloat16 [256, 128, 1024], P('tm', 'freq')
- input_grad: bfloat16 [256, 128, 1024], P('tm', 'freq')
- weight_grads: float32 [1024, 4, 1024], P(('tm', 'freq'))
The draws below stay inside these ranges and needn't reach their ends.
All inputs are finite; a program needn't handle non-finite values.
Results may differ from the reference program's by a relative error of at most 0.0093.
Values may be sent and summed in bfloat16 or wider, within the bound.
No kernel may reach another device: no remote copies, remote signals or barrier semaphores. Data moves between devices by JAX's collectives and lax.ppermute only.
A program may use at most 256 MiB of HBM per device.

```python
import math
import jax
import jax.numpy as jnp
from jax import lax

D = 1024
HEADS = 8
TIME = 256
FREQ = 128


def draw_tokens(key, part):
    base_key = jax.random.fold_in(key, 101)
    scale_key = jax.random.fold_in(key, 102)
    feature_scale = 0.5 * jnp.exp(jax.random.uniform(scale_key, (D,), jnp.float32, 0.0, math.log(10.0)))
    field = jax.random.normal(base_key, (TIME, FREQ, D), jnp.float32) * feature_scale
    return jnp.clip(field, -16.0, 16.0).astype(jnp.bfloat16)


def paired_weight(key, which):
    own = jax.random.normal(jax.random.fold_in(key, 202 + which), (D, D), jnp.float32)
    matrix = own
    return jnp.clip(matrix * D ** (-0.5), -1.0, 1.0).astype(jnp.bfloat16)


def draw_w_query(key, part):
    return paired_weight(key, 0)


def draw_w_key(key, part):
    return paired_weight(key, 1)


def block_scale(own_key, dims, split, least, largest):
    def one(position, parts):
        steps = jax.random.uniform(jax.random.fold_in(jax.random.fold_in(own_key, 6), position), (parts,), jnp.float32, least / len(split), largest / len(split))
        return jnp.repeat(jnp.exp(steps), dims[position] // parts).reshape((-1,) + (1,) * (len(dims) - position - 1))

    gain = one(*split[0])
    for cut in split[1:]:
        gain = gain * one(*cut)
    return gain


def centred(rng, extent, width, most, split=(), kind=jnp.bfloat16):
    drawn = jax.random.normal(rng, extent, jnp.float32) * width
    if len(split) > 0:
        drawn = block_scale(rng, extent, split, -0.22, 0.18) * drawn
    return jnp.clip(drawn, min=-most, max=most).astype(kind)


def setup_inputs(seed: int = 0) -> dict:
    arg_keys = jax.random.split(jax.random.key(seed), 7)
    tokens = draw_tokens(jax.random.fold_in(arg_keys[6], 71), 0)
    w_query = draw_w_query(jax.random.fold_in(arg_keys[6], 71), 0)
    w_key = draw_w_key(jax.random.fold_in(arg_keys[6], 71), 0)
    w_value = centred(arg_keys[3], (D, D), D ** -0.5, 0.1875)
    w_out = centred(arg_keys[4], (D, D), (D // 16) ** -0.5, 0.75)
    d_out = centred(arg_keys[5], (TIME, FREQ, D), 1.0, 6.0, ((0, 16), (1, 8)))
    return dict(tokens=tokens, w_query=w_query, w_key=w_key, w_value=w_value, w_out=w_out, d_out=d_out)


window_reach = 6
tile_edge = 8
span_edge = 20
norm_eps = 1e-05
far_value = -1e+30

def mix(form, left_operand, right_operand):
    return jnp.einsum(form, left_operand.astype(jnp.float32), right_operand.astype(jnp.float32))

def window_mask():
    query_pos = jnp.arange(tile_edge * tile_edge)
    key_pos = jnp.arange(span_edge * span_edge)
    rise_rows = (key_pos // span_edge)[None, :] - (query_pos // tile_edge)[:, None]
    rise_cols = (key_pos % span_edge)[None, :] - (query_pos % tile_edge)[:, None]
    return (rise_rows >= 0) & (rise_rows <= 2 * window_reach) & (rise_cols >= 0) & (rise_cols <= 2 * window_reach)

def pack_tiles(field_map):
    row_total, col_total = (field_map.shape[0], field_map.shape[1])
    trailing = field_map.shape[2:]
    shaped = field_map.reshape((row_total // tile_edge, tile_edge, col_total // tile_edge, tile_edge) + trailing)
    axes_order = (0, 2, 1, 3) + tuple(range(4, shaped.ndim))
    return shaped.transpose(axes_order).reshape((row_total // tile_edge * (col_total // tile_edge), tile_edge * tile_edge) + trailing)

def unpack_tiles(tile_stack, row_total, col_total):
    trailing = tile_stack.shape[2:]
    shaped = tile_stack.reshape((row_total // tile_edge, col_total // tile_edge, tile_edge, tile_edge) + trailing)
    axes_order = (0, 2, 1, 3) + tuple(range(4, shaped.ndim))
    return shaped.transpose(axes_order).reshape((row_total, col_total) + trailing)

def spread_tiles(field_map, row_total, col_total):
    trailing = field_map.shape[2:]
    tile_rows = row_total // tile_edge
    tile_cols = col_total // tile_edge
    row_index = (tile_edge * jnp.arange(tile_rows))[:, None] + jnp.arange(span_edge)[None, :]
    col_index = (tile_edge * jnp.arange(tile_cols))[:, None] + jnp.arange(span_edge)[None, :]
    picked = jnp.take(field_map, row_index, axis=0)
    picked = jnp.take(picked, col_index, axis=2)
    axes_order = (0, 2, 1, 3) + tuple(range(4, picked.ndim))
    return picked.transpose(axes_order).reshape((tile_rows * tile_cols, span_edge * span_edge) + trailing)

def group_size(tile_count):
    best_width = 1
    for candidate in range(1, 9):
        if tile_count % candidate == 0:
            best_width = candidate
    return best_width

def over_groups(group_func, members):
    tile_count = members[0].shape[0]
    best_width = group_size(tile_count)
    grouped = tuple((member.reshape((tile_count // best_width, best_width) + member.shape[1:]) for member in members))
    results = lax.map(lambda group_parts: group_func(*group_parts), grouped)
    return tuple((member.reshape((tile_count,) + member.shape[2:]) for member in results))

def attend_forward(query_map, key_map, value_map, key_ok, head_count):
    row_total, col_total, model_width = query_map.shape
    head_dim = model_width // head_count
    score_scale = 1.0 / math.sqrt(head_dim)
    inside = window_mask()
    q_tiles = pack_tiles(query_map).reshape(-1, tile_edge * tile_edge, head_count, head_dim)
    k_tiles = spread_tiles(key_map, row_total, col_total).reshape(-1, span_edge * span_edge, head_count, head_dim)
    v_tiles = spread_tiles(value_map, row_total, col_total).reshape(-1, span_edge * span_edge, head_count, head_dim)
    ok_tiles = spread_tiles(key_ok, row_total, col_total)

    def one_group(q_part, k_part, v_part, ok_part):
        allowed = inside[None, None] & (ok_part[:, None, None, :] > 0.5)
        scores = mix('nqhd,nkhd->nhqk', q_part, k_part) * score_scale
        scores = jnp.where(allowed, scores, far_value)
        row_max = lax.optimization_barrier(jnp.max(scores, axis=-1, keepdims=True))
        log_total = row_max + jnp.log(lax.optimization_barrier(jnp.sum(jnp.exp(scores - row_max), axis=-1, keepdims=True)))
        soft_weights = jnp.where(allowed, jnp.exp(scores - log_total), 0.0)
        attended = mix('nhqk,nkhd->nqhd', soft_weights.astype(jnp.bfloat16), v_part)
        return (attended, log_total[..., 0])
    attended, log_total = over_groups(one_group, (q_tiles, k_tiles, v_tiles, ok_tiles))
    attended = unpack_tiles(attended.reshape(-1, tile_edge * tile_edge, model_width), row_total, col_total)
    log_total = unpack_tiles(log_total.transpose(0, 2, 1), row_total, col_total)
    return (attended, log_total)

def attend_query_grad(query_map, key_map, value_map, key_ok, grad_map, head_count):
    row_total, col_total, model_width = query_map.shape
    head_dim = model_width // head_count
    score_scale = 1.0 / math.sqrt(head_dim)
    inside = window_mask()
    q_tiles = pack_tiles(query_map).reshape(-1, tile_edge * tile_edge, head_count, head_dim)
    g_tiles = pack_tiles(grad_map).reshape(-1, tile_edge * tile_edge, head_count, head_dim)
    k_tiles = spread_tiles(key_map, row_total, col_total).reshape(-1, span_edge * span_edge, head_count, head_dim)
    v_tiles = spread_tiles(value_map, row_total, col_total).reshape(-1, span_edge * span_edge, head_count, head_dim)
    ok_tiles = spread_tiles(key_ok, row_total, col_total)

    def one_group(q_part, g_part, k_part, v_part, ok_part):
        allowed = inside[None, None] & (ok_part[:, None, None, :] > 0.5)
        scores = mix('nqhd,nkhd->nhqk', q_part, k_part) * score_scale
        scores = jnp.where(allowed, scores, far_value)
        row_max = lax.optimization_barrier(jnp.max(scores, axis=-1, keepdims=True))
        log_total = row_max + jnp.log(lax.optimization_barrier(jnp.sum(jnp.exp(scores - row_max), axis=-1, keepdims=True)))
        soft_weights = jnp.where(allowed, jnp.exp(scores - log_total), 0.0)
        grad_probs = mix('nqhd,nkhd->nhqk', g_part, v_part)
        spread = lax.optimization_barrier(jnp.sum(soft_weights * grad_probs, axis=-1, keepdims=True))
        grad_scores = (soft_weights * (grad_probs - spread) * score_scale).astype(jnp.bfloat16)
        grad_query = mix('nhqk,nkhd->nqhd', grad_scores, k_part)
        return (grad_query, log_total[..., 0], spread[..., 0])
    grad_query, log_total, spread = over_groups(one_group, (q_tiles, g_tiles, k_tiles, v_tiles, ok_tiles))
    grad_query = unpack_tiles(grad_query.reshape(-1, tile_edge * tile_edge, model_width), row_total, col_total)
    log_total = unpack_tiles(log_total.transpose(0, 2, 1), row_total, col_total)
    spread = unpack_tiles(spread.transpose(0, 2, 1), row_total, col_total)
    return (grad_query, log_total, spread)

def attend_key_grad(key_map, value_map, query_map, grad_map, log_total, spread, head_count):
    row_total, col_total, model_width = key_map.shape
    head_dim = model_width // head_count
    score_scale = 1.0 / math.sqrt(head_dim)
    inside = window_mask()
    k_tiles = pack_tiles(key_map).reshape(-1, tile_edge * tile_edge, head_count, head_dim)
    v_tiles = pack_tiles(value_map).reshape(-1, tile_edge * tile_edge, head_count, head_dim)
    q_tiles = spread_tiles(query_map, row_total, col_total).reshape(-1, span_edge * span_edge, head_count, head_dim)
    g_tiles = spread_tiles(grad_map, row_total, col_total).reshape(-1, span_edge * span_edge, head_count, head_dim)
    l_tiles = spread_tiles(log_total, row_total, col_total).transpose(0, 2, 1)
    s_tiles = spread_tiles(spread, row_total, col_total).transpose(0, 2, 1)

    def one_group(k_part, v_part, q_part, g_part, l_part, s_part):
        scores = mix('nkhd,nqhd->nhkq', k_part, q_part) * score_scale
        soft_weights = jnp.where(inside[None, None], jnp.exp(scores - l_part[:, :, None, :]), 0.0)
        grad_probs = mix('nkhd,nqhd->nhkq', v_part, g_part)
        grad_scores = (soft_weights * (grad_probs - s_part[:, :, None, :]) * score_scale).astype(jnp.bfloat16)
        grad_keys = mix('nhkq,nqhd->nkhd', grad_scores, q_part)
        grad_values = mix('nhkq,nqhd->nkhd', soft_weights.astype(jnp.bfloat16), g_part)
        return (grad_keys, grad_values)
    grad_keys, grad_values = over_groups(one_group, (k_tiles, v_tiles, q_tiles, g_tiles, l_tiles, s_tiles))
    grad_keys = unpack_tiles(grad_keys.reshape(-1, tile_edge * tile_edge, model_width), row_total, col_total)
    grad_values = unpack_tiles(grad_values.reshape(-1, tile_edge * tile_edge, model_width), row_total, col_total)
    return (grad_keys, grad_values)

def layer_norm(flat_rows):
    wide_values = flat_rows.astype(jnp.float32)
    center = lax.optimization_barrier(jnp.mean(wide_values, axis=-1, keepdims=True))
    shifted = wide_values - center
    inverse = lax.rsqrt(lax.optimization_barrier(jnp.mean(shifted * shifted, axis=-1, keepdims=True)) + norm_eps)
    return (shifted * inverse, inverse)

def pad_map(field_map, margin):
    return jnp.pad(field_map, ((margin, margin), (margin, margin)) + ((0, 0),) * (field_map.ndim - 2))

def reference(tokens, w_query, w_key, w_value, w_out, d_out):
    time_all, freq_all, model_width = tokens.shape
    flat_rows = tokens.reshape(-1, model_width)
    normed, inverse = layer_norm(flat_rows)
    hidden = normed.astype(jnp.bfloat16)
    query_rows = jnp.dot(hidden, w_query, preferred_element_type=jnp.float32).astype(jnp.bfloat16)
    key_rows = jnp.dot(hidden, w_key, preferred_element_type=jnp.float32).astype(jnp.bfloat16)
    value_rows = jnp.dot(hidden, w_value, preferred_element_type=jnp.float32).astype(jnp.bfloat16)
    query_map = query_rows.reshape(time_all, freq_all, model_width)
    key_pad = pad_map(key_rows.reshape(time_all, freq_all, model_width), window_reach)
    value_pad = pad_map(value_rows.reshape(time_all, freq_all, model_width), window_reach)
    ok_pad = pad_map(jnp.ones((time_all, freq_all), jnp.float32), window_reach)
    band_ids = jnp.arange(time_all // tile_edge, dtype=jnp.int32)

    def forward_band(band):
        row_start = (band * tile_edge).astype(jnp.int32)
        q_band = lax.dynamic_slice_in_dim(query_map, row_start, tile_edge, 0)
        k_band = lax.dynamic_slice_in_dim(key_pad, row_start, span_edge, 0)
        v_band = lax.dynamic_slice_in_dim(value_pad, row_start, span_edge, 0)
        ok_band = lax.dynamic_slice_in_dim(ok_pad, row_start, span_edge, 0)
        attended, unused = attend_forward(q_band, k_band, v_band, ok_band, HEADS)
        return attended.astype(jnp.bfloat16)
    attended_rows = lax.map(forward_band, band_ids).reshape(-1, model_width)
    output = (flat_rows.astype(jnp.float32) + jnp.dot(attended_rows, w_out, preferred_element_type=jnp.float32)).astype(jnp.bfloat16)
    grad_flat = d_out.reshape(-1, model_width)
    grad_att = jnp.dot(grad_flat, w_out.T, preferred_element_type=jnp.float32).astype(jnp.bfloat16)
    grad_map = grad_att.reshape(time_all, freq_all, model_width)

    def query_band(band):
        row_start = (band * tile_edge).astype(jnp.int32)
        q_band = lax.dynamic_slice_in_dim(query_map, row_start, tile_edge, 0)
        g_band = lax.dynamic_slice_in_dim(grad_map, row_start, tile_edge, 0)
        k_band = lax.dynamic_slice_in_dim(key_pad, row_start, span_edge, 0)
        v_band = lax.dynamic_slice_in_dim(value_pad, row_start, span_edge, 0)
        ok_band = lax.dynamic_slice_in_dim(ok_pad, row_start, span_edge, 0)
        grad_query, log_total, spread = attend_query_grad(q_band, k_band, v_band, ok_band, g_band, HEADS)
        return (grad_query.astype(jnp.bfloat16), log_total, spread)
    grad_query, log_total, spread = lax.map(query_band, band_ids)
    grad_query = grad_query.reshape(-1, model_width)
    log_pad = pad_map(log_total.reshape(time_all, freq_all, -1), window_reach)
    spread_pad = pad_map(spread.reshape(time_all, freq_all, -1), window_reach)
    query_pad = pad_map(query_map, window_reach)
    grad_pad = pad_map(grad_map, window_reach)
    key_map = key_rows.reshape(time_all, freq_all, model_width)
    value_map = value_rows.reshape(time_all, freq_all, model_width)

    def key_band(band):
        row_start = (band * tile_edge).astype(jnp.int32)
        k_band = lax.dynamic_slice_in_dim(key_map, row_start, tile_edge, 0)
        v_band = lax.dynamic_slice_in_dim(value_map, row_start, tile_edge, 0)
        q_band = lax.dynamic_slice_in_dim(query_pad, row_start, span_edge, 0)
        g_band = lax.dynamic_slice_in_dim(grad_pad, row_start, span_edge, 0)
        l_band = lax.dynamic_slice_in_dim(log_pad, row_start, span_edge, 0)
        s_band = lax.dynamic_slice_in_dim(spread_pad, row_start, span_edge, 0)
        grad_keys, grad_values = attend_key_grad(k_band, v_band, q_band, g_band, l_band, s_band, HEADS)
        return (grad_keys.astype(jnp.bfloat16), grad_values.astype(jnp.bfloat16))
    grad_keys, grad_values = lax.map(key_band, band_ids)
    grad_keys = grad_keys.reshape(-1, model_width)
    grad_values = grad_values.reshape(-1, model_width)
    weight_grads = jnp.stack([jnp.dot(hidden.T, grad_query, preferred_element_type=jnp.float32), jnp.dot(hidden.T, grad_keys, preferred_element_type=jnp.float32), jnp.dot(hidden.T, grad_values, preferred_element_type=jnp.float32), jnp.dot(attended_rows.T, grad_flat, preferred_element_type=jnp.float32)], axis=1)
    grad_hidden = jnp.dot(grad_query, w_query.T, preferred_element_type=jnp.float32)
    grad_hidden = grad_hidden + jnp.dot(grad_keys, w_key.T, preferred_element_type=jnp.float32)
    grad_hidden = grad_hidden + jnp.dot(grad_values, w_value.T, preferred_element_type=jnp.float32)
    center_grad = lax.optimization_barrier(jnp.mean(grad_hidden, axis=-1, keepdims=True))
    along = lax.optimization_barrier(jnp.mean(grad_hidden * normed, axis=-1, keepdims=True))
    input_grad = (grad_flat.astype(jnp.float32) + (grad_hidden - center_grad - normed * along) * inverse).astype(jnp.bfloat16)
    return (output.reshape(time_all, freq_all, model_width), input_grad.reshape(time_all, freq_all, model_width), weight_grads)
```

```python
import math

import jax
import jax.numpy as jnp
from jax import lax
from jax.sharding import PartitionSpec as P

HEADS = 8


window_reach = 6
tile_edge = 8
span_edge = 20
norm_eps = 1e-05
far_value = -1e30


def extended(array, sides, width):
    for axis, dim in sides:
        size, length = (lax.axis_size(axis), array.shape[dim])
        up = [(i, (i + 1) % size) for i in range(size - 1)]
        down = [(j, i) for i, j in up]
        last = lax.slice_in_dim(array, length - width, length, axis=dim)
        leading = lax.slice_in_dim(array, 0, width, axis=dim)
        before = lax.ppermute(last, axis, up)
        after = lax.ppermute(leading, axis, down)
        array = jnp.concatenate([before, array, after], axis=dim)
    return array


def mix(form, left_operand, right_operand):
    return jnp.einsum(form, left_operand, right_operand, preferred_element_type=jnp.float32)


def window_mask():
    query_pos = jnp.arange(tile_edge * tile_edge)
    key_pos = jnp.arange(span_edge * span_edge)
    rise_rows = (key_pos // span_edge)[None, :] - (query_pos // tile_edge)[:, None]
    rise_cols = (key_pos % span_edge)[None, :] - (query_pos % tile_edge)[:, None]
    return (
        (rise_rows >= 0)
        & (rise_rows <= 2 * window_reach)
        & (rise_cols >= 0)
        & (rise_cols <= 2 * window_reach)
    )


def pack_tiles(field_map):
    row_total, col_total = (field_map.shape[0], field_map.shape[1])
    trailing = field_map.shape[2:]
    shaped = field_map.reshape(
        (row_total // tile_edge, tile_edge, col_total // tile_edge, tile_edge) + trailing
    )
    axes_order = (0, 2, 1, 3) + tuple(range(4, shaped.ndim))
    return shaped.transpose(axes_order).reshape(
        (row_total // tile_edge * (col_total // tile_edge), tile_edge * tile_edge) + trailing
    )


def unpack_tiles(tile_stack, row_total, col_total):
    trailing = tile_stack.shape[2:]
    shaped = tile_stack.reshape(
        (row_total // tile_edge, col_total // tile_edge, tile_edge, tile_edge) + trailing
    )
    axes_order = (0, 2, 1, 3) + tuple(range(4, shaped.ndim))
    return shaped.transpose(axes_order).reshape((row_total, col_total) + trailing)


def spread_tiles(field_map, row_total, col_total):
    trailing = field_map.shape[2:]
    tile_rows = row_total // tile_edge
    tile_cols = col_total // tile_edge
    row_index = (tile_edge * jnp.arange(tile_rows))[:, None] + jnp.arange(span_edge)[None, :]
    col_index = (tile_edge * jnp.arange(tile_cols))[:, None] + jnp.arange(span_edge)[None, :]
    picked = jnp.take(field_map, row_index, axis=0)
    picked = jnp.take(picked, col_index, axis=2)
    axes_order = (0, 2, 1, 3) + tuple(range(4, picked.ndim))
    return picked.transpose(axes_order).reshape(
        (tile_rows * tile_cols, span_edge * span_edge) + trailing
    )


def group_size(tile_count):
    best_width = 1
    for candidate in range(1, 9):
        if tile_count % candidate == 0:
            best_width = candidate
    return best_width


def over_groups(group_func, members):
    tile_count = members[0].shape[0]
    best_width = group_size(tile_count)
    grouped = tuple(
        (
            member.reshape((tile_count // best_width, best_width) + member.shape[1:])
            for member in members
        )
    )
    results = lax.map(lambda group_parts: group_func(*group_parts), grouped)
    return tuple((member.reshape((tile_count,) + member.shape[2:]) for member in results))


def attend_forward(query_map, key_map, value_map, key_ok, head_count):
    row_total, col_total, model_width = query_map.shape
    head_dim = model_width // head_count
    score_scale = 1.0 / math.sqrt(head_dim)
    inside = window_mask()
    q_tiles = pack_tiles(query_map).reshape(-1, tile_edge * tile_edge, head_count, head_dim)
    k_tiles = spread_tiles(key_map, row_total, col_total).reshape(
        -1, span_edge * span_edge, head_count, head_dim
    )
    v_tiles = spread_tiles(value_map, row_total, col_total).reshape(
        -1, span_edge * span_edge, head_count, head_dim
    )
    ok_tiles = spread_tiles(key_ok, row_total, col_total)

    def one_group(q_part, k_part, v_part, ok_part):
        allowed = inside[None, None] & (ok_part[:, None, None, :] > 0.5)
        scores = mix("nqhd,nkhd->nhqk", q_part, k_part) * score_scale
        scores = jnp.where(allowed, scores, far_value)
        row_max = jnp.max(scores, axis=-1, keepdims=True)
        log_total = row_max + jnp.log(jnp.sum(jnp.exp(scores - row_max), axis=-1, keepdims=True))
        soft_weights = jnp.where(allowed, jnp.exp(scores - log_total), 0.0)
        attended = mix("nhqk,nkhd->nqhd", soft_weights.astype(jnp.bfloat16), v_part)
        return (attended, log_total[..., 0])

    attended, log_total = over_groups(one_group, (q_tiles, k_tiles, v_tiles, ok_tiles))
    attended = unpack_tiles(
        attended.reshape(-1, tile_edge * tile_edge, model_width), row_total, col_total
    )
    log_total = unpack_tiles(log_total.transpose(0, 2, 1), row_total, col_total)
    return (attended, log_total)


def attend_query_grad(query_map, key_map, value_map, key_ok, grad_map, head_count):
    row_total, col_total, model_width = query_map.shape
    head_dim = model_width // head_count
    score_scale = 1.0 / math.sqrt(head_dim)
    inside = window_mask()
    q_tiles = pack_tiles(query_map).reshape(-1, tile_edge * tile_edge, head_count, head_dim)
    g_tiles = pack_tiles(grad_map).reshape(-1, tile_edge * tile_edge, head_count, head_dim)
    k_tiles = spread_tiles(key_map, row_total, col_total).reshape(
        -1, span_edge * span_edge, head_count, head_dim
    )
    v_tiles = spread_tiles(value_map, row_total, col_total).reshape(
        -1, span_edge * span_edge, head_count, head_dim
    )
    ok_tiles = spread_tiles(key_ok, row_total, col_total)

    def one_group(q_part, g_part, k_part, v_part, ok_part):
        allowed = inside[None, None] & (ok_part[:, None, None, :] > 0.5)
        scores = mix("nqhd,nkhd->nhqk", q_part, k_part) * score_scale
        scores = jnp.where(allowed, scores, far_value)
        row_max = jnp.max(scores, axis=-1, keepdims=True)
        log_total = row_max + jnp.log(jnp.sum(jnp.exp(scores - row_max), axis=-1, keepdims=True))
        soft_weights = jnp.where(allowed, jnp.exp(scores - log_total), 0.0)
        grad_probs = mix("nqhd,nkhd->nhqk", g_part, v_part)
        spread = jnp.sum(soft_weights * grad_probs, axis=-1, keepdims=True)
        grad_scores = (soft_weights * (grad_probs - spread) * score_scale).astype(jnp.bfloat16)
        grad_query = mix("nhqk,nkhd->nqhd", grad_scores, k_part)
        return (grad_query, log_total[..., 0], spread[..., 0])

    grad_query, log_total, spread = over_groups(
        one_group, (q_tiles, g_tiles, k_tiles, v_tiles, ok_tiles)
    )
    grad_query = unpack_tiles(
        grad_query.reshape(-1, tile_edge * tile_edge, model_width), row_total, col_total
    )
    log_total = unpack_tiles(log_total.transpose(0, 2, 1), row_total, col_total)
    spread = unpack_tiles(spread.transpose(0, 2, 1), row_total, col_total)
    return (grad_query, log_total, spread)


def attend_key_grad(key_map, value_map, query_map, grad_map, log_total, spread, head_count):
    row_total, col_total, model_width = key_map.shape
    head_dim = model_width // head_count
    score_scale = 1.0 / math.sqrt(head_dim)
    inside = window_mask()
    k_tiles = pack_tiles(key_map).reshape(-1, tile_edge * tile_edge, head_count, head_dim)
    v_tiles = pack_tiles(value_map).reshape(-1, tile_edge * tile_edge, head_count, head_dim)
    q_tiles = spread_tiles(query_map, row_total, col_total).reshape(
        -1, span_edge * span_edge, head_count, head_dim
    )
    g_tiles = spread_tiles(grad_map, row_total, col_total).reshape(
        -1, span_edge * span_edge, head_count, head_dim
    )
    l_tiles = spread_tiles(log_total, row_total, col_total).transpose(0, 2, 1)
    s_tiles = spread_tiles(spread, row_total, col_total).transpose(0, 2, 1)

    def one_group(k_part, v_part, q_part, g_part, l_part, s_part):
        scores = mix("nkhd,nqhd->nhkq", k_part, q_part) * score_scale
        soft_weights = jnp.where(inside[None, None], jnp.exp(scores - l_part[:, :, None, :]), 0.0)
        grad_probs = mix("nkhd,nqhd->nhkq", v_part, g_part)
        grad_scores = (soft_weights * (grad_probs - s_part[:, :, None, :]) * score_scale).astype(
            jnp.bfloat16
        )
        grad_keys = mix("nhkq,nqhd->nkhd", grad_scores, q_part)
        grad_values = mix("nhkq,nqhd->nkhd", soft_weights.astype(jnp.bfloat16), g_part)
        return (grad_keys, grad_values)

    grad_keys, grad_values = over_groups(
        one_group, (k_tiles, v_tiles, q_tiles, g_tiles, l_tiles, s_tiles)
    )
    grad_keys = unpack_tiles(
        grad_keys.reshape(-1, tile_edge * tile_edge, model_width), row_total, col_total
    )
    grad_values = unpack_tiles(
        grad_values.reshape(-1, tile_edge * tile_edge, model_width), row_total, col_total
    )
    return (grad_keys, grad_values)


def layer_norm(flat_rows):
    wide_values = flat_rows.astype(jnp.float32)
    center = jnp.mean(wide_values, axis=-1, keepdims=True)
    shifted = wide_values - center
    inverse = lax.rsqrt(jnp.mean(shifted * shifted, axis=-1, keepdims=True) + norm_eps)
    return (shifted * inverse, inverse)


def local(tokens, w_query, w_key, w_value, w_out, d_out):
    tile_rows, tile_cols, model_width = tokens.shape
    flat_rows = tokens.reshape(tile_rows * tile_cols, model_width)
    normed, inverse = layer_norm(flat_rows)
    hidden = normed.astype(jnp.bfloat16)
    query_rows = jnp.dot(hidden, w_query, preferred_element_type=jnp.float32).astype(jnp.bfloat16)
    key_rows = jnp.dot(hidden, w_key, preferred_element_type=jnp.float32).astype(jnp.bfloat16)
    value_rows = jnp.dot(hidden, w_value, preferred_element_type=jnp.float32).astype(jnp.bfloat16)
    query_map = query_rows.reshape(tile_rows, tile_cols, model_width)
    key_map = key_rows.reshape(tile_rows, tile_cols, model_width)
    value_map = value_rows.reshape(tile_rows, tile_cols, model_width)
    time_all = tile_rows * lax.axis_size("tm")
    freq_all = tile_cols * lax.axis_size("freq")
    time_start = lax.axis_index("tm") * tile_rows
    freq_start = lax.axis_index("freq") * tile_cols

    def inside_map(margin):
        time_pos = time_start - margin + jnp.arange(tile_rows + 2 * margin)
        freq_pos = freq_start - margin + jnp.arange(tile_cols + 2 * margin)
        time_ok = (time_pos >= 0) & (time_pos < time_all)
        freq_ok = (freq_pos >= 0) & (freq_pos < freq_all)
        return (time_ok[:, None] & freq_ok[None, :]).astype(jnp.float32)

    kv_pair = jnp.stack([key_map, value_map])
    near_rim = extended(kv_pair, (("tm", 1), ("freq", 2)), 6)
    attended, unused = attend_forward(query_map, near_rim[0], near_rim[1], inside_map(6), HEADS)
    attended_rows = attended.astype(jnp.bfloat16).reshape(tile_rows * tile_cols, model_width)
    output = (
        flat_rows.astype(jnp.float32)
        + jnp.dot(attended_rows, w_out, preferred_element_type=jnp.float32)
    ).astype(jnp.bfloat16)
    grad_flat = d_out.reshape(tile_rows * tile_cols, model_width)
    grad_att = jnp.dot(grad_flat, w_out.T, preferred_element_type=jnp.float32).astype(jnp.bfloat16)
    grad_att_map = grad_att.reshape(tile_rows, tile_cols, model_width)
    query_pair = jnp.stack([query_map, grad_att_map])
    beside_all = extended(query_pair, (("tm", 1), ("freq", 2)), 6)
    grad_query_tile, log_own, spread_own = attend_query_grad(
        query_map, near_rim[0], near_rim[1], inside_map(6), grad_att_map, HEADS
    )
    grad_query = grad_query_tile.astype(jnp.bfloat16).reshape(tile_rows * tile_cols, model_width)
    stats_pair = extended(jnp.stack([log_own, spread_own]), (("tm", 1), ("freq", 2)), 6)
    log_rim = stats_pair[0]
    spread_rim = stats_pair[1]
    grad_keys, grad_values = attend_key_grad(
        key_map, value_map, beside_all[0], beside_all[1], log_rim, spread_rim, HEADS
    )
    grad_keys = grad_keys.astype(jnp.bfloat16).reshape(tile_rows * tile_cols, model_width)
    grad_values = grad_values.astype(jnp.bfloat16).reshape(tile_rows * tile_cols, model_width)
    contract_dims = (((0,), (0,)), ((), ()))

    def scatter_rows(term):
        return lax.psum_scatter(term, ("tm", "freq"), scatter_dimension=0, tiled=True)

    out_term = scatter_rows(
        lax.dot_general(attended_rows, grad_flat, contract_dims, preferred_element_type=jnp.float32)
    )
    query_term = scatter_rows(
        lax.dot_general(hidden, grad_query, contract_dims, preferred_element_type=jnp.float32)
    )
    kv_rows = jnp.concatenate([grad_keys, grad_values], axis=1)
    kv_term = scatter_rows(
        lax.dot_general(hidden, kv_rows, contract_dims, preferred_element_type=jnp.float32)
    )
    weight_grads = jnp.stack(
        [query_term, kv_term[:, :model_width], kv_term[:, model_width:], out_term], axis=1
    )
    grad_hidden = jnp.dot(grad_query, w_query.T, preferred_element_type=jnp.float32)
    grad_hidden = grad_hidden + jnp.dot(grad_keys, w_key.T, preferred_element_type=jnp.float32)
    grad_hidden = grad_hidden + jnp.dot(grad_values, w_value.T, preferred_element_type=jnp.float32)
    center_grad = jnp.mean(grad_hidden, axis=-1, keepdims=True)
    along = jnp.mean(grad_hidden * normed, axis=-1, keepdims=True)
    input_grad = (
        grad_flat.astype(jnp.float32) + (grad_hidden - center_grad - normed * along) * inverse
    ).astype(jnp.bfloat16)
    return (
        output.reshape(tile_rows, tile_cols, model_width),
        input_grad.reshape(tile_rows, tile_cols, model_width),
        weight_grads,
    )


def solution(mesh):
    in_specs = (P("tm", "freq", None), P(), P(), P(), P(), P("tm", "freq", None))
    out_specs = (P("tm", "freq", None), P("tm", "freq", None), P(("tm", "freq"), None, None))
    return jax.shard_map(local, mesh=mesh, in_specs=in_specs, out_specs=out_specs, check_vma=False)
```

```python
import math

import jax
import jax.numpy as jnp
from jax import lax
from jax.sharding import PartitionSpec as P

HEADS = 8


window_reach = 6
tile_edge = 8
span_edge = 20
norm_eps = 1e-05
far_value = -1e30


def extended(array, sides, width):
    for axis, dim in sides:
        size, length = (lax.axis_size(axis), array.shape[dim])
        up = [(i, (i + 1) % size) for i in range(size - 1)]
        down = [(j, i) for i, j in up]
        last = lax.slice_in_dim(array, length - width, length, axis=dim)
        leading = lax.slice_in_dim(array, 0, width, axis=dim)
        before = lax.ppermute(last, axis, up)
        after = lax.ppermute(leading, axis, down)
        array = jnp.concatenate([before, array, after], axis=dim)
    return array


def mix(form, left_operand, right_operand):
    return jnp.einsum(form, left_operand, right_operand, preferred_element_type=jnp.float32)


def window_mask():
    query_pos = jnp.arange(tile_edge * tile_edge)
    key_pos = jnp.arange(span_edge * span_edge)
    rise_rows = (key_pos // span_edge)[None, :] - (query_pos // tile_edge)[:, None]
    rise_cols = (key_pos % span_edge)[None, :] - (query_pos % tile_edge)[:, None]
    return (
        (rise_rows >= 0)
        & (rise_rows <= 2 * window_reach)
        & (rise_cols >= 0)
        & (rise_cols <= 2 * window_reach)
    )


def pack_tiles(field_map):
    row_total, col_total = (field_map.shape[0], field_map.shape[1])
    trailing = field_map.shape[2:]
    shaped = field_map.reshape(
        (row_total // tile_edge, tile_edge, col_total // tile_edge, tile_edge) + trailing
    )
    axes_order = (0, 2, 1, 3) + tuple(range(4, shaped.ndim))
    return shaped.transpose(axes_order).reshape(
        (row_total // tile_edge * (col_total // tile_edge), tile_edge * tile_edge) + trailing
    )


def unpack_tiles(tile_stack, row_total, col_total):
    trailing = tile_stack.shape[2:]
    shaped = tile_stack.reshape(
        (row_total // tile_edge, col_total // tile_edge, tile_edge, tile_edge) + trailing
    )
    axes_order = (0, 2, 1, 3) + tuple(range(4, shaped.ndim))
    return shaped.transpose(axes_order).reshape((row_total, col_total) + trailing)


def spread_tiles(field_map, row_total, col_total):
    trailing = field_map.shape[2:]
    tile_rows = row_total // tile_edge
    tile_cols = col_total // tile_edge
    row_index = (tile_edge * jnp.arange(tile_rows))[:, None] + jnp.arange(span_edge)[None, :]
    col_index = (tile_edge * jnp.arange(tile_cols))[:, None] + jnp.arange(span_edge)[None, :]
    picked = jnp.take(field_map, row_index, axis=0)
    picked = jnp.take(picked, col_index, axis=2)
    axes_order = (0, 2, 1, 3) + tuple(range(4, picked.ndim))
    return picked.transpose(axes_order).reshape(
        (tile_rows * tile_cols, span_edge * span_edge) + trailing
    )


def group_size(tile_count):
    best_width = 1
    for candidate in range(1, 9):
        if tile_count % candidate == 0:
            best_width = candidate
    return best_width


def over_groups(group_func, members):
    tile_count = members[0].shape[0]
    best_width = group_size(tile_count)
    grouped = tuple(
        (
            member.reshape((tile_count // best_width, best_width) + member.shape[1:])
            for member in members
        )
    )
    results = lax.map(lambda group_parts: group_func(*group_parts), grouped)
    return tuple((member.reshape((tile_count,) + member.shape[2:]) for member in results))


def attend_forward(query_map, key_map, value_map, key_ok, head_count):
    row_total, col_total, model_width = query_map.shape
    head_dim = model_width // head_count
    score_scale = 1.0 / math.sqrt(head_dim)
    inside = window_mask()
    q_tiles = pack_tiles(query_map).reshape(-1, tile_edge * tile_edge, head_count, head_dim)
    k_tiles = spread_tiles(key_map, row_total, col_total).reshape(
        -1, span_edge * span_edge, head_count, head_dim
    )
    v_tiles = spread_tiles(value_map, row_total, col_total).reshape(
        -1, span_edge * span_edge, head_count, head_dim
    )
    ok_tiles = spread_tiles(key_ok, row_total, col_total)

    def one_group(q_part, k_part, v_part, ok_part):
        allowed = inside[None, None] & (ok_part[:, None, None, :] > 0.5)
        scores = mix("nqhd,nkhd->nhqk", q_part, k_part) * score_scale
        scores = jnp.where(allowed, scores, far_value)
        row_max = jnp.max(scores, axis=-1, keepdims=True)
        log_total = row_max + jnp.log(jnp.sum(jnp.exp(scores - row_max), axis=-1, keepdims=True))
        soft_weights = jnp.where(allowed, jnp.exp(scores - log_total), 0.0)
        attended = mix("nhqk,nkhd->nqhd", soft_weights.astype(jnp.bfloat16), v_part)
        return (attended, log_total[..., 0])

    attended, log_total = over_groups(one_group, (q_tiles, k_tiles, v_tiles, ok_tiles))
    attended = unpack_tiles(
        attended.reshape(-1, tile_edge * tile_edge, model_width), row_total, col_total
    )
    log_total = unpack_tiles(log_total.transpose(0, 2, 1), row_total, col_total)
    return (attended, log_total)


def attend_query_grad(query_map, key_map, value_map, key_ok, grad_map, head_count):
    row_total, col_total, model_width = query_map.shape
    head_dim = model_width // head_count
    score_scale = 1.0 / math.sqrt(head_dim)
    inside = window_mask()
    q_tiles = pack_tiles(query_map).reshape(-1, tile_edge * tile_edge, head_count, head_dim)
    g_tiles = pack_tiles(grad_map).reshape(-1, tile_edge * tile_edge, head_count, head_dim)
    k_tiles = spread_tiles(key_map, row_total, col_total).reshape(
        -1, span_edge * span_edge, head_count, head_dim
    )
    v_tiles = spread_tiles(value_map, row_total, col_total).reshape(
        -1, span_edge * span_edge, head_count, head_dim
    )
    ok_tiles = spread_tiles(key_ok, row_total, col_total)

    def one_group(q_part, g_part, k_part, v_part, ok_part):
        allowed = inside[None, None] & (ok_part[:, None, None, :] > 0.5)
        scores = mix("nqhd,nkhd->nhqk", q_part, k_part) * score_scale
        scores = jnp.where(allowed, scores, far_value)
        row_max = jnp.max(scores, axis=-1, keepdims=True)
        log_total = row_max + jnp.log(jnp.sum(jnp.exp(scores - row_max), axis=-1, keepdims=True))
        soft_weights = jnp.where(allowed, jnp.exp(scores - log_total), 0.0)
        grad_probs = mix("nqhd,nkhd->nhqk", g_part, v_part)
        spread = jnp.sum(soft_weights * grad_probs, axis=-1, keepdims=True)
        grad_scores = (soft_weights * (grad_probs - spread) * score_scale).astype(jnp.bfloat16)
        grad_query = mix("nhqk,nkhd->nqhd", grad_scores, k_part)
        return (grad_query, log_total[..., 0], spread[..., 0])

    grad_query, log_total, spread = over_groups(
        one_group, (q_tiles, g_tiles, k_tiles, v_tiles, ok_tiles)
    )
    grad_query = unpack_tiles(
        grad_query.reshape(-1, tile_edge * tile_edge, model_width), row_total, col_total
    )
    log_total = unpack_tiles(log_total.transpose(0, 2, 1), row_total, col_total)
    spread = unpack_tiles(spread.transpose(0, 2, 1), row_total, col_total)
    return (grad_query, log_total, spread)


def attend_key_grad(key_map, value_map, query_map, grad_map, log_total, spread, head_count):
    row_total, col_total, model_width = key_map.shape
    head_dim = model_width // head_count
    score_scale = 1.0 / math.sqrt(head_dim)
    inside = window_mask()
    k_tiles = pack_tiles(key_map).reshape(-1, tile_edge * tile_edge, head_count, head_dim)
    v_tiles = pack_tiles(value_map).reshape(-1, tile_edge * tile_edge, head_count, head_dim)
    q_tiles = spread_tiles(query_map, row_total, col_total).reshape(
        -1, span_edge * span_edge, head_count, head_dim
    )
    g_tiles = spread_tiles(grad_map, row_total, col_total).reshape(
        -1, span_edge * span_edge, head_count, head_dim
    )
    l_tiles = spread_tiles(log_total, row_total, col_total).transpose(0, 2, 1)
    s_tiles = spread_tiles(spread, row_total, col_total).transpose(0, 2, 1)

    def one_group(k_part, v_part, q_part, g_part, l_part, s_part):
        scores = mix("nkhd,nqhd->nhkq", k_part, q_part) * score_scale
        soft_weights = jnp.where(inside[None, None], jnp.exp(scores - l_part[:, :, None, :]), 0.0)
        grad_probs = mix("nkhd,nqhd->nhkq", v_part, g_part)
        grad_scores = (soft_weights * (grad_probs - s_part[:, :, None, :]) * score_scale).astype(
            jnp.bfloat16
        )
        grad_keys = mix("nhkq,nqhd->nkhd", grad_scores, q_part)
        grad_values = mix("nhkq,nqhd->nkhd", soft_weights.astype(jnp.bfloat16), g_part)
        return (grad_keys, grad_values)

    grad_keys, grad_values = over_groups(
        one_group, (k_tiles, v_tiles, q_tiles, g_tiles, l_tiles, s_tiles)
    )
    grad_keys = unpack_tiles(
        grad_keys.reshape(-1, tile_edge * tile_edge, model_width), row_total, col_total
    )
    grad_values = unpack_tiles(
        grad_values.reshape(-1, tile_edge * tile_edge, model_width), row_total, col_total
    )
    return (grad_keys, grad_values)


def layer_norm(flat_rows):
    wide_values = flat_rows.astype(jnp.float32)
    center = jnp.mean(wide_values, axis=-1, keepdims=True)
    shifted = wide_values - center
    inverse = lax.rsqrt(jnp.mean(shifted * shifted, axis=-1, keepdims=True) + norm_eps)
    return (shifted * inverse, inverse)


def local(tokens, w_query, w_key, w_value, w_out, d_out):
    tile_rows, tile_cols, model_width = tokens.shape
    flat_rows = tokens.reshape(tile_rows * tile_cols, model_width)
    normed, inverse = layer_norm(flat_rows)
    hidden = normed.astype(jnp.bfloat16)
    query_rows = jnp.dot(hidden, w_query, preferred_element_type=jnp.float32).astype(jnp.bfloat16)
    key_rows = jnp.dot(hidden, w_key, preferred_element_type=jnp.float32).astype(jnp.bfloat16)
    value_rows = jnp.dot(hidden, w_value, preferred_element_type=jnp.float32).astype(jnp.bfloat16)
    query_map = query_rows.reshape(tile_rows, tile_cols, model_width)
    key_map = key_rows.reshape(tile_rows, tile_cols, model_width)
    value_map = value_rows.reshape(tile_rows, tile_cols, model_width)
    time_all = tile_rows * lax.axis_size("tm")
    freq_all = tile_cols * lax.axis_size("freq")
    time_start = lax.axis_index("tm") * tile_rows
    freq_start = lax.axis_index("freq") * tile_cols

    def inside_map(margin):
        time_pos = time_start - margin + jnp.arange(tile_rows + 2 * margin)
        freq_pos = freq_start - margin + jnp.arange(tile_cols + 2 * margin)
        time_ok = (time_pos >= 0) & (time_pos < time_all)
        freq_ok = (freq_pos >= 0) & (freq_pos < freq_all)
        return (time_ok[:, None] & freq_ok[None, :]).astype(jnp.float32)

    kv_pair = jnp.stack([key_map, value_map])
    near_rim = extended(kv_pair, (("tm", 1), ("freq", 2)), 6)
    attended, unused = attend_forward(query_map, near_rim[0], near_rim[1], inside_map(6), HEADS)
    attended_rows = attended.astype(jnp.bfloat16).reshape(tile_rows * tile_cols, model_width)
    output = (
        flat_rows.astype(jnp.float32)
        + jnp.dot(attended_rows, w_out, preferred_element_type=jnp.float32)
    ).astype(jnp.bfloat16)
    grad_flat = d_out.reshape(tile_rows * tile_cols, model_width)
    grad_att = jnp.dot(grad_flat, w_out.T, preferred_element_type=jnp.float32).astype(jnp.bfloat16)
    grad_att_map = grad_att.reshape(tile_rows, tile_cols, model_width)
    query_pair = jnp.stack([query_map, grad_att_map])
    beside_all = extended(query_pair, (("tm", 1), ("freq", 2)), 6)
    grad_query_tile, log_own, spread_own = attend_query_grad(
        query_map, near_rim[0], near_rim[1], inside_map(6), grad_att_map, HEADS
    )
    grad_query = grad_query_tile.astype(jnp.bfloat16).reshape(tile_rows * tile_cols, model_width)
    stats_pair = extended(jnp.stack([log_own, spread_own]), (("tm", 1), ("freq", 2)), 6)
    log_rim = stats_pair[0]
    spread_rim = stats_pair[1]
    grad_keys, grad_values = attend_key_grad(
        key_map, value_map, beside_all[0], beside_all[1], log_rim, spread_rim, HEADS
    )
    grad_keys = grad_keys.astype(jnp.bfloat16).reshape(tile_rows * tile_cols, model_width)
    grad_values = grad_values.astype(jnp.bfloat16).reshape(tile_rows * tile_cols, model_width)
    contract_dims = (((0,), (0,)), ((), ()))
    hidden_rows = jnp.concatenate([grad_query, grad_keys, grad_values], axis=1)
    term_rows = jnp.concatenate(
        [
            lax.dot_general(hidden, hidden_rows, contract_dims, preferred_element_type=jnp.float32),
            lax.dot_general(
                attended_rows, grad_flat, contract_dims, preferred_element_type=jnp.float32
            ),
        ],
        axis=1,
    )
    summed = lax.psum(term_rows, ("tm", "freq"))
    row_count = model_width // (lax.axis_size("tm") * lax.axis_size("freq"))
    row_start = (lax.axis_index("tm") * lax.axis_size("freq") + lax.axis_index("freq")) * row_count
    weight_grads = lax.dynamic_slice_in_dim(summed, row_start, row_count, axis=0).reshape(
        row_count, 4, model_width
    )
    grad_hidden = jnp.dot(grad_query, w_query.T, preferred_element_type=jnp.float32)
    grad_hidden = grad_hidden + jnp.dot(grad_keys, w_key.T, preferred_element_type=jnp.float32)
    grad_hidden = grad_hidden + jnp.dot(grad_values, w_value.T, preferred_element_type=jnp.float32)
    center_grad = jnp.mean(grad_hidden, axis=-1, keepdims=True)
    along = jnp.mean(grad_hidden * normed, axis=-1, keepdims=True)
    input_grad = (
        grad_flat.astype(jnp.float32) + (grad_hidden - center_grad - normed * along) * inverse
    ).astype(jnp.bfloat16)
    return (
        output.reshape(tile_rows, tile_cols, model_width),
        input_grad.reshape(tile_rows, tile_cols, model_width),
        weight_grads,
    )


def solution(mesh):
    in_specs = (P("tm", "freq", None), P(), P(), P(), P(), P("tm", "freq", None))
    out_specs = (P("tm", "freq", None), P("tm", "freq", None), P(("tm", "freq"), None, None))
    return jax.shard_map(local, mesh=mesh, in_specs=in_specs, out_specs=out_specs, check_vma=False)
```

```python
import math

import jax
import jax.numpy as jnp
from jax import lax
from jax.sharding import PartitionSpec as P

HEADS = 8


window_reach = 6
tile_edge = 8
span_edge = 20
norm_eps = 1e-05
far_value = -1e30


def extended(array, sides, width):
    for axis, dim in sides:
        size, length = (lax.axis_size(axis), array.shape[dim])
        up = [(i, (i + 1) % size) for i in range(size - 1)]
        down = [(j, i) for i, j in up]
        last = lax.slice_in_dim(array, length - width, length, axis=dim)
        leading = lax.slice_in_dim(array, 0, width, axis=dim)
        before = lax.ppermute(last, axis, up)
        after = lax.ppermute(leading, axis, down)
        array = jnp.concatenate([before, array, after], axis=dim)
    return array


def mix(form, left_operand, right_operand):
    return jnp.einsum(form, left_operand, right_operand, preferred_element_type=jnp.float32)


def window_mask():
    query_pos = jnp.arange(tile_edge * tile_edge)
    key_pos = jnp.arange(span_edge * span_edge)
    rise_rows = (key_pos // span_edge)[None, :] - (query_pos // tile_edge)[:, None]
    rise_cols = (key_pos % span_edge)[None, :] - (query_pos % tile_edge)[:, None]
    return (
        (rise_rows >= 0)
        & (rise_rows <= 2 * window_reach)
        & (rise_cols >= 0)
        & (rise_cols <= 2 * window_reach)
    )


def pack_tiles(field_map):
    lead, row_total, col_total = field_map.shape[:3]
    trailing = field_map.shape[3:]
    shaped = field_map.reshape(
        (lead, row_total // tile_edge, tile_edge, col_total // tile_edge, tile_edge) + trailing
    )
    axes_order = (0, 1, 3, 2, 4) + tuple(range(5, shaped.ndim))
    return shaped.transpose(axes_order).reshape(
        (lead, row_total // tile_edge * (col_total // tile_edge), tile_edge * tile_edge)
        + trailing
    )


def unpack_tiles(tile_stack, row_total, col_total):
    lead = tile_stack.shape[0]
    trailing = tile_stack.shape[3:]
    shaped = tile_stack.reshape(
        (lead, row_total // tile_edge, col_total // tile_edge, tile_edge, tile_edge) + trailing
    )
    axes_order = (0, 1, 3, 2, 4) + tuple(range(5, shaped.ndim))
    return shaped.transpose(axes_order).reshape((lead, row_total, col_total) + trailing)


def spread_tiles(field_map, row_total, col_total):
    lead = field_map.shape[0]
    trailing = field_map.shape[3:]
    spans = []
    for tile_row in range(row_total // tile_edge):
        for tile_col in range(col_total // tile_edge):
            row_at, col_at = tile_row * tile_edge, tile_col * tile_edge
            spans.append(
                field_map[:, row_at : row_at + span_edge, col_at : col_at + span_edge].reshape(
                    (lead, span_edge * span_edge) + trailing
                )
            )
    return jnp.stack(spans, axis=1)


def attend_both(q_heads, k_rim, v_rim, g_heads, key_ok, head_count):
    head_count, row_total, col_total, head_dim = q_heads.shape
    score_scale = 1.0 / math.sqrt(head_dim)
    inside = window_mask()
    q_part = pack_tiles(q_heads)
    g_part = pack_tiles(g_heads)
    k_part = spread_tiles(k_rim, row_total, col_total)
    v_part = spread_tiles(v_rim, row_total, col_total)
    ok_part = spread_tiles(key_ok[None], row_total, col_total)[0]
    allowed = inside[None, None] & (ok_part[None, :, None, :] > 0.5)
    scores = mix("hnqd,hnkd->hnqk", q_part, k_part) * score_scale
    scores = jnp.where(allowed, scores, far_value)
    row_max = jnp.max(scores, axis=-1, keepdims=True)
    log_total = row_max + jnp.log(jnp.sum(jnp.exp(scores - row_max), axis=-1, keepdims=True))
    soft_weights = jnp.where(allowed, jnp.exp(scores - log_total), 0.0)
    attended = mix("hnqk,hnkd->hnqd", soft_weights.astype(jnp.bfloat16), v_part)
    grad_probs = mix("hnqd,hnkd->hnqk", g_part, v_part)
    spread = jnp.sum(soft_weights * grad_probs, axis=-1, keepdims=True)
    grad_scores = (soft_weights * (grad_probs - spread) * score_scale).astype(jnp.bfloat16)
    grad_query = mix("hnqk,hnkd->hnqd", grad_scores, k_part)
    return (
        unpack_tiles(attended.astype(jnp.bfloat16), row_total, col_total),
        unpack_tiles(grad_query.astype(jnp.bfloat16), row_total, col_total),
        unpack_tiles(log_total[..., 0], row_total, col_total),
        unpack_tiles(spread[..., 0], row_total, col_total),
    )


def attend_key_grad(k_heads, v_heads, q_rim, g_rim, log_rim, spread_rim, head_count):
    head_count, row_total, col_total, head_dim = k_heads.shape
    score_scale = 1.0 / math.sqrt(head_dim)
    inside = window_mask()
    k_part = pack_tiles(k_heads)
    v_part = pack_tiles(v_heads)
    q_part = spread_tiles(q_rim, row_total, col_total)
    g_part = spread_tiles(g_rim, row_total, col_total)
    l_part = spread_tiles(log_rim, row_total, col_total)
    s_part = spread_tiles(spread_rim, row_total, col_total)
    scores = mix("hnkd,hnqd->hnkq", k_part, q_part) * score_scale
    soft_weights = jnp.where(inside[None, None], jnp.exp(scores - l_part[:, :, None, :]), 0.0)
    grad_probs = mix("hnkd,hnqd->hnkq", v_part, g_part)
    grad_scores = (soft_weights * (grad_probs - s_part[:, :, None, :]) * score_scale).astype(
        jnp.bfloat16
    )
    grad_keys = mix("hnkq,hnqd->hnkd", grad_scores, q_part)
    grad_values = mix("hnkq,hnqd->hnkd", soft_weights.astype(jnp.bfloat16), g_part)
    return (
        unpack_tiles(grad_keys.astype(jnp.bfloat16), row_total, col_total),
        unpack_tiles(grad_values.astype(jnp.bfloat16), row_total, col_total),
    )


def layer_norm(flat_rows):
    wide_values = flat_rows.astype(jnp.float32)
    center = jnp.mean(wide_values, axis=-1, keepdims=True)
    shifted = wide_values - center
    inverse = lax.rsqrt(jnp.mean(shifted * shifted, axis=-1, keepdims=True) + norm_eps)
    return (shifted * inverse, inverse)


def local(tokens, w_query, w_key, w_value, w_out, d_out):
    tile_rows, tile_cols, model_width = tokens.shape
    head_dim = model_width // HEADS
    token_count = tile_rows * tile_cols
    flat_rows = tokens.reshape(token_count, model_width)
    normed, inverse = layer_norm(flat_rows)
    hidden = normed.astype(jnp.bfloat16)

    def split_heads(weight):
        return weight.reshape(model_width, HEADS, head_dim)

    def project(weight):
        rows = mix("td,dhe->hte", hidden, split_heads(weight)).astype(jnp.bfloat16)
        return rows.reshape(HEADS, tile_rows, tile_cols, head_dim)

    q_heads = project(w_query)
    k_heads = project(w_key)
    v_heads = project(w_value)
    grad_flat = d_out.reshape(token_count, model_width)
    out_heads = w_out.reshape(HEADS, head_dim, model_width)
    g_heads = mix("tf,hef->hte", grad_flat, out_heads).astype(jnp.bfloat16)
    g_heads = g_heads.reshape(HEADS, tile_rows, tile_cols, head_dim)
    time_all = tile_rows * lax.axis_size("tm")
    freq_all = tile_cols * lax.axis_size("freq")
    time_start = lax.axis_index("tm") * tile_rows
    freq_start = lax.axis_index("freq") * tile_cols

    def inside_map(margin):
        time_pos = time_start - margin + jnp.arange(tile_rows + 2 * margin)
        freq_pos = freq_start - margin + jnp.arange(tile_cols + 2 * margin)
        time_ok = (time_pos >= 0) & (time_pos < time_all)
        freq_ok = (freq_pos >= 0) & (freq_pos < freq_all)
        return (time_ok[:, None] & freq_ok[None, :]).astype(jnp.float32)

    sides = (("tm", 2), ("freq", 3))
    near_rim = extended(jnp.stack([k_heads, v_heads]), sides, window_reach)
    beside_all = extended(jnp.stack([q_heads, g_heads]), sides, window_reach)
    attended, grad_query, log_own, spread_own = attend_both(
        q_heads, near_rim[0], near_rim[1], g_heads, inside_map(window_reach), HEADS
    )
    stats_rim = extended(jnp.stack([log_own, spread_own]), sides, window_reach)
    grad_keys, grad_values = attend_key_grad(
        k_heads, v_heads, beside_all[0], beside_all[1], stats_rim[0], stats_rim[1], HEADS
    )
    attended = attended.reshape(HEADS, token_count, head_dim)
    grad_query = grad_query.reshape(HEADS, token_count, head_dim)
    grad_keys = grad_keys.reshape(HEADS, token_count, head_dim)
    grad_values = grad_values.reshape(HEADS, token_count, head_dim)
    output = (flat_rows.astype(jnp.float32) + mix("hte,hef->tf", attended, out_heads)).astype(
        jnp.bfloat16
    )

    def weight_term(grad_heads):
        return mix("td,hte->dhe", hidden, grad_heads).reshape(model_width, model_width)

    term_rows = jnp.concatenate(
        [
            weight_term(grad_query),
            weight_term(grad_keys),
            weight_term(grad_values),
            mix("hte,tf->hef", attended, grad_flat).reshape(model_width, model_width),
        ],
        axis=1,
    )
    summed = lax.psum(term_rows, ("tm", "freq"))
    row_count = model_width // (lax.axis_size("tm") * lax.axis_size("freq"))
    row_start = (lax.axis_index("tm") * lax.axis_size("freq") + lax.axis_index("freq")) * row_count
    weight_grads = lax.dynamic_slice_in_dim(summed, row_start, row_count, axis=0).reshape(
        row_count, 4, model_width
    )
    grad_hidden = mix("hte,dhe->td", grad_query, split_heads(w_query))
    grad_hidden = grad_hidden + mix("hte,dhe->td", grad_keys, split_heads(w_key))
    grad_hidden = grad_hidden + mix("hte,dhe->td", grad_values, split_heads(w_value))
    center_grad = jnp.mean(grad_hidden, axis=-1, keepdims=True)
    along = jnp.mean(grad_hidden * normed, axis=-1, keepdims=True)
    input_grad = (
        grad_flat.astype(jnp.float32) + (grad_hidden - center_grad - normed * along) * inverse
    ).astype(jnp.bfloat16)
    return (
        output.reshape(tile_rows, tile_cols, model_width),
        input_grad.reshape(tile_rows, tile_cols, model_width),
        weight_grads,
    )


def solution(mesh):
    in_specs = (P("tm", "freq", None), P(), P(), P(), P(), P("tm", "freq", None))
    out_specs = (P("tm", "freq", None), P("tm", "freq", None), P(("tm", "freq"), None, None))
    return jax.shard_map(local, mesh=mesh, in_specs=in_specs, out_specs=out_specs, check_vma=False)
```

```python
import math

import jax
import jax.numpy as jnp
from jax import lax
from jax.sharding import Mesh, PartitionSpec as P

HEADS = 8
TIME_AXES = ("tz", "core")


window_reach = 6
tile_edge = 8
span_edge = 20
norm_eps = 1e-05
far_value = -1e30


def extended(array, sides, width):
    for axis, dim in sides:
        size, length = (lax.axis_size(axis), array.shape[dim])
        up = [(i, (i + 1) % size) for i in range(size - 1)]
        down = [(j, i) for i, j in up]
        last = lax.slice_in_dim(array, length - width, length, axis=dim)
        leading = lax.slice_in_dim(array, 0, width, axis=dim)
        before = lax.ppermute(last, axis, up)
        after = lax.ppermute(leading, axis, down)
        array = jnp.concatenate([before, array, after], axis=dim)
    return array


def mix(form, left_operand, right_operand):
    return jnp.einsum(form, left_operand, right_operand, preferred_element_type=jnp.float32)


def window_mask():
    query_pos = jnp.arange(tile_edge * tile_edge)
    key_pos = jnp.arange(span_edge * span_edge)
    rise_rows = (key_pos // span_edge)[None, :] - (query_pos // tile_edge)[:, None]
    rise_cols = (key_pos % span_edge)[None, :] - (query_pos % tile_edge)[:, None]
    return (
        (rise_rows >= 0)
        & (rise_rows <= 2 * window_reach)
        & (rise_cols >= 0)
        & (rise_cols <= 2 * window_reach)
    )


def pack_tiles(field_map):
    lead, row_total, col_total = field_map.shape[:3]
    trailing = field_map.shape[3:]
    shaped = field_map.reshape(
        (lead, row_total // tile_edge, tile_edge, col_total // tile_edge, tile_edge) + trailing
    )
    axes_order = (0, 1, 3, 2, 4) + tuple(range(5, shaped.ndim))
    return shaped.transpose(axes_order).reshape(
        (lead, row_total // tile_edge * (col_total // tile_edge), tile_edge * tile_edge)
        + trailing
    )


def unpack_tiles(tile_stack, row_total, col_total):
    lead = tile_stack.shape[0]
    trailing = tile_stack.shape[3:]
    shaped = tile_stack.reshape(
        (lead, row_total // tile_edge, col_total // tile_edge, tile_edge, tile_edge) + trailing
    )
    axes_order = (0, 1, 3, 2, 4) + tuple(range(5, shaped.ndim))
    return shaped.transpose(axes_order).reshape((lead, row_total, col_total) + trailing)


def spread_tiles(field_map, row_total, col_total):
    lead = field_map.shape[0]
    trailing = field_map.shape[3:]
    spans = []
    for tile_row in range(row_total // tile_edge):
        for tile_col in range(col_total // tile_edge):
            row_at, col_at = tile_row * tile_edge, tile_col * tile_edge
            spans.append(
                field_map[:, row_at : row_at + span_edge, col_at : col_at + span_edge].reshape(
                    (lead, span_edge * span_edge) + trailing
                )
            )
    return jnp.stack(spans, axis=1)


def attend_both(q_heads, k_rim, v_rim, g_heads, key_ok, head_count):
    head_count, row_total, col_total, head_dim = q_heads.shape
    score_scale = 1.0 / math.sqrt(head_dim)
    inside = window_mask()
    q_part = pack_tiles(q_heads)
    g_part = pack_tiles(g_heads)
    k_part = spread_tiles(k_rim, row_total, col_total)
    v_part = spread_tiles(v_rim, row_total, col_total)
    ok_part = spread_tiles(key_ok[None], row_total, col_total)[0]
    allowed = inside[None, None] & (ok_part[None, :, None, :] > 0.5)
    scores = mix("hnqd,hnkd->hnqk", q_part, k_part) * score_scale
    scores = jnp.where(allowed, scores, far_value)
    row_max = jnp.max(scores, axis=-1, keepdims=True)
    log_total = row_max + jnp.log(jnp.sum(jnp.exp(scores - row_max), axis=-1, keepdims=True))
    soft_weights = jnp.where(allowed, jnp.exp(scores - log_total), 0.0)
    attended = mix("hnqk,hnkd->hnqd", soft_weights.astype(jnp.bfloat16), v_part)
    grad_probs = mix("hnqd,hnkd->hnqk", g_part, v_part)
    spread = jnp.sum(soft_weights * grad_probs, axis=-1, keepdims=True)
    grad_scores = (soft_weights * (grad_probs - spread) * score_scale).astype(jnp.bfloat16)
    grad_query = mix("hnqk,hnkd->hnqd", grad_scores, k_part)
    return (
        unpack_tiles(attended.astype(jnp.bfloat16), row_total, col_total),
        unpack_tiles(grad_query.astype(jnp.bfloat16), row_total, col_total),
        unpack_tiles(log_total[..., 0], row_total, col_total),
        unpack_tiles(spread[..., 0], row_total, col_total),
    )


def attend_key_grad(k_heads, v_heads, q_rim, g_rim, log_rim, spread_rim, head_count):
    head_count, row_total, col_total, head_dim = k_heads.shape
    score_scale = 1.0 / math.sqrt(head_dim)
    inside = window_mask()
    k_part = pack_tiles(k_heads)
    v_part = pack_tiles(v_heads)
    q_part = spread_tiles(q_rim, row_total, col_total)
    g_part = spread_tiles(g_rim, row_total, col_total)
    l_part = spread_tiles(log_rim, row_total, col_total)
    s_part = spread_tiles(spread_rim, row_total, col_total)
    scores = mix("hnkd,hnqd->hnkq", k_part, q_part) * score_scale
    soft_weights = jnp.where(inside[None, None], jnp.exp(scores - l_part[:, :, None, :]), 0.0)
    grad_probs = mix("hnkd,hnqd->hnkq", v_part, g_part)
    grad_scores = (soft_weights * (grad_probs - s_part[:, :, None, :]) * score_scale).astype(
        jnp.bfloat16
    )
    grad_keys = mix("hnkq,hnqd->hnkd", grad_scores, q_part)
    grad_values = mix("hnkq,hnqd->hnkd", soft_weights.astype(jnp.bfloat16), g_part)
    return (
        unpack_tiles(grad_keys.astype(jnp.bfloat16), row_total, col_total),
        unpack_tiles(grad_values.astype(jnp.bfloat16), row_total, col_total),
    )


def layer_norm(flat_rows):
    wide_values = flat_rows.astype(jnp.float32)
    center = jnp.mean(wide_values, axis=-1, keepdims=True)
    shifted = wide_values - center
    inverse = lax.rsqrt(jnp.mean(shifted * shifted, axis=-1, keepdims=True) + norm_eps)
    return (shifted * inverse, inverse)


def local(tokens, w_query, w_key, w_value, w_out, d_out):
    tile_rows, tile_cols, model_width = tokens.shape
    head_dim = model_width // HEADS
    token_count = tile_rows * tile_cols
    flat_rows = tokens.reshape(token_count, model_width)
    normed, inverse = layer_norm(flat_rows)
    hidden = normed.astype(jnp.bfloat16)

    def split_heads(weight):
        return weight.reshape(model_width, HEADS, head_dim)

    def project(weight):
        rows = mix("td,dhe->hte", hidden, split_heads(weight)).astype(jnp.bfloat16)
        return rows.reshape(HEADS, tile_rows, tile_cols, head_dim)

    q_heads = project(w_query)
    k_heads = project(w_key)
    v_heads = project(w_value)
    grad_flat = d_out.reshape(token_count, model_width)
    out_heads = w_out.reshape(HEADS, head_dim, model_width)
    g_heads = mix("tf,hef->hte", grad_flat, out_heads).astype(jnp.bfloat16)
    g_heads = g_heads.reshape(HEADS, tile_rows, tile_cols, head_dim)
    time_all = tile_rows * lax.axis_size(TIME_AXES)
    freq_all = tile_cols * lax.axis_size("freq")
    time_start = lax.axis_index(TIME_AXES) * tile_rows
    freq_start = lax.axis_index("freq") * tile_cols

    def inside_map(margin):
        time_pos = time_start - margin + jnp.arange(tile_rows + 2 * margin)
        freq_pos = freq_start - margin + jnp.arange(tile_cols + 2 * margin)
        time_ok = (time_pos >= 0) & (time_pos < time_all)
        freq_ok = (freq_pos >= 0) & (freq_pos < freq_all)
        return (time_ok[:, None] & freq_ok[None, :]).astype(jnp.float32)

    sides = ((TIME_AXES, 2), ("freq", 3))
    near_rim = extended(jnp.stack([k_heads, v_heads]), sides, window_reach)
    beside_all = extended(jnp.stack([q_heads, g_heads]), sides, window_reach)
    attended, grad_query, log_own, spread_own = attend_both(
        q_heads, near_rim[0], near_rim[1], g_heads, inside_map(window_reach), HEADS
    )
    stats_rim = extended(jnp.stack([log_own, spread_own]), sides, window_reach)
    grad_keys, grad_values = attend_key_grad(
        k_heads, v_heads, beside_all[0], beside_all[1], stats_rim[0], stats_rim[1], HEADS
    )
    attended = attended.reshape(HEADS, token_count, head_dim)
    grad_query = grad_query.reshape(HEADS, token_count, head_dim)
    grad_keys = grad_keys.reshape(HEADS, token_count, head_dim)
    grad_values = grad_values.reshape(HEADS, token_count, head_dim)
    output = (flat_rows.astype(jnp.float32) + mix("hte,hef->tf", attended, out_heads)).astype(
        jnp.bfloat16
    )

    core = lax.axis_index("core")
    pair = [(0, 1), (1, 0)]
    hidden_split = hidden.reshape(token_count, HEADS, 2, head_dim // 2)
    attended_split = attended.reshape(HEADS, token_count, 2, head_dim // 2)
    hidden_mine = lax.dynamic_index_in_dim(hidden_split, core, axis=2, keepdims=False)
    hidden_theirs = lax.dynamic_index_in_dim(hidden_split, 1 - core, axis=2, keepdims=False)
    attended_mine = lax.dynamic_index_in_dim(attended_split, core, axis=2, keepdims=False)
    attended_theirs = lax.dynamic_index_in_dim(attended_split, 1 - core, axis=2, keepdims=False)
    hidden_got, attended_got, query_got, keys_got, values_got, grad_got = lax.ppermute(
        (hidden_theirs, attended_theirs, grad_query, grad_keys, grad_values, grad_flat),
        "core",
        pair,
    )
    hidden_both = jnp.concatenate([hidden_mine, hidden_got], axis=0)
    attended_both = jnp.concatenate([attended_mine, attended_got], axis=1)
    grad_both = jnp.concatenate([grad_flat, grad_got], axis=0)
    half_rows = model_width // 2

    def weight_term(grad_heads, grad_heads_got):
        both = jnp.concatenate([grad_heads, grad_heads_got], axis=1)
        return mix("tab,hte->abhe", hidden_both, both).reshape(half_rows, model_width)

    term_rows = jnp.concatenate(
        [
            weight_term(grad_query, query_got),
            weight_term(grad_keys, keys_got),
            weight_term(grad_values, values_got),
            mix("atb,tf->abf", attended_both, grad_both).reshape(half_rows, model_width),
        ],
        axis=1,
    )
    summed = lax.psum(term_rows, ("tz", "freq"))
    row_count = model_width // (lax.axis_size(TIME_AXES) * lax.axis_size("freq"))
    row_start = (lax.axis_index("tz") * lax.axis_size("freq") + lax.axis_index("freq")) * row_count
    weight_grads = lax.dynamic_slice_in_dim(summed, row_start, row_count, axis=0).reshape(
        row_count, 4, model_width
    )
    grad_hidden = mix("hte,dhe->td", grad_query, split_heads(w_query))
    grad_hidden = grad_hidden + mix("hte,dhe->td", grad_keys, split_heads(w_key))
    grad_hidden = grad_hidden + mix("hte,dhe->td", grad_values, split_heads(w_value))
    center_grad = jnp.mean(grad_hidden, axis=-1, keepdims=True)
    along = jnp.mean(grad_hidden * normed, axis=-1, keepdims=True)
    input_grad = (
        grad_flat.astype(jnp.float32) + (grad_hidden - center_grad - normed * along) * inverse
    ).astype(jnp.bfloat16)
    return (
        output.reshape(tile_rows, tile_cols, model_width),
        input_grad.reshape(tile_rows, tile_cols, model_width),
        weight_grads,
    )


def solution(mesh):
    time_size, freq_size = mesh.shape["tm"], mesh.shape["freq"]
    inner = Mesh(mesh.devices.reshape(time_size // 2, 2, freq_size), ("tz", "core", "freq"))
    in_specs = (P(TIME_AXES, "freq", None), P(), P(), P(), P(), P(TIME_AXES, "freq", None))
    out_specs = (
        P(TIME_AXES, "freq", None),
        P(TIME_AXES, "freq", None),
        P(("tz", "core", "freq"), None, None),
    )
    return jax.shard_map(local, mesh=inner, in_specs=in_specs, out_specs=out_specs, check_vma=False)
```

```python
import math

import jax
import jax.numpy as jnp
from jax import lax
from jax.sharding import Mesh, PartitionSpec as P

HEADS = 8
TIME_AXES = ("tz", "core")


window_reach = 6
tile_edge = 8
span_edge = 20
norm_eps = 1e-05
far_value = -1e30


def extended(array, sides, width):
    for axis, dim in sides:
        size, length = (lax.axis_size(axis), array.shape[dim])
        up = [(i, (i + 1) % size) for i in range(size - 1)]
        down = [(j, i) for i, j in up]
        last = lax.slice_in_dim(array, length - width, length, axis=dim)
        leading = lax.slice_in_dim(array, 0, width, axis=dim)
        before = lax.ppermute(last, axis, up)
        after = lax.ppermute(leading, axis, down)
        array = jnp.concatenate([before, array, after], axis=dim)
    return array


def mix(form, left_operand, right_operand):
    return jnp.einsum(form, left_operand, right_operand, preferred_element_type=jnp.float32)


def window_mask():
    query_pos = jnp.arange(tile_edge * tile_edge)
    key_pos = jnp.arange(span_edge * span_edge)
    rise_rows = (key_pos // span_edge)[None, :] - (query_pos // tile_edge)[:, None]
    rise_cols = (key_pos % span_edge)[None, :] - (query_pos % tile_edge)[:, None]
    return (
        (rise_rows >= 0)
        & (rise_rows <= 2 * window_reach)
        & (rise_cols >= 0)
        & (rise_cols <= 2 * window_reach)
    )


def pack_tiles(field_map):
    lead, row_total, col_total = field_map.shape[:3]
    trailing = field_map.shape[3:]
    shaped = field_map.reshape(
        (lead, row_total // tile_edge, tile_edge, col_total // tile_edge, tile_edge) + trailing
    )
    axes_order = (0, 1, 3, 2, 4) + tuple(range(5, shaped.ndim))
    return shaped.transpose(axes_order).reshape(
        (lead, row_total // tile_edge * (col_total // tile_edge), tile_edge * tile_edge)
        + trailing
    )


def unpack_tiles(tile_stack, row_total, col_total):
    lead = tile_stack.shape[0]
    trailing = tile_stack.shape[3:]
    shaped = tile_stack.reshape(
        (lead, row_total // tile_edge, col_total // tile_edge, tile_edge, tile_edge) + trailing
    )
    axes_order = (0, 1, 3, 2, 4) + tuple(range(5, shaped.ndim))
    return shaped.transpose(axes_order).reshape((lead, row_total, col_total) + trailing)


def spread_tiles(field_map, row_total, col_total):
    lead = field_map.shape[0]
    trailing = field_map.shape[3:]
    spans = []
    for tile_row in range(row_total // tile_edge):
        for tile_col in range(col_total // tile_edge):
            row_at, col_at = tile_row * tile_edge, tile_col * tile_edge
            spans.append(
                field_map[:, row_at : row_at + span_edge, col_at : col_at + span_edge].reshape(
                    (lead, span_edge * span_edge) + trailing
                )
            )
    return jnp.stack(spans, axis=1)


def attend_both(q_heads, k_rim, v_rim, g_heads, key_ok, head_count):
    head_count, row_total, col_total, head_dim = q_heads.shape
    score_scale = 1.0 / math.sqrt(head_dim)
    inside = window_mask()
    q_part = pack_tiles(q_heads)
    g_part = pack_tiles(g_heads)
    k_part = spread_tiles(k_rim, row_total, col_total)
    v_part = spread_tiles(v_rim, row_total, col_total)
    ok_part = spread_tiles(key_ok[None], row_total, col_total)[0]
    allowed = inside[None, None] & (ok_part[None, :, None, :] > 0.5)
    scores = mix("hnqd,hnkd->hnqk", q_part, k_part) * score_scale
    scores = jnp.where(allowed, scores, far_value)
    row_max = jnp.max(scores, axis=-1, keepdims=True)
    log_total = row_max + jnp.log(jnp.sum(jnp.exp(scores - row_max), axis=-1, keepdims=True))
    soft_weights = jnp.where(allowed, jnp.exp(scores - log_total), 0.0)
    attended = mix("hnqk,hnkd->hnqd", soft_weights.astype(jnp.bfloat16), v_part)
    grad_probs = mix("hnqd,hnkd->hnqk", g_part, v_part)
    spread = jnp.sum(soft_weights * grad_probs, axis=-1, keepdims=True)
    grad_scores = (soft_weights * (grad_probs - spread) * score_scale).astype(jnp.bfloat16)
    grad_query = mix("hnqk,hnkd->hnqd", grad_scores, k_part)
    return (
        unpack_tiles(attended.astype(jnp.bfloat16), row_total, col_total),
        unpack_tiles(grad_query.astype(jnp.bfloat16), row_total, col_total),
        unpack_tiles(log_total[..., 0], row_total, col_total),
        unpack_tiles(spread[..., 0], row_total, col_total),
    )


def attend_key_grad(k_heads, v_heads, q_rim, g_rim, log_rim, spread_rim, head_count):
    head_count, row_total, col_total, head_dim = k_heads.shape
    score_scale = 1.0 / math.sqrt(head_dim)
    inside = window_mask()
    k_part = pack_tiles(k_heads)
    v_part = pack_tiles(v_heads)
    q_part = spread_tiles(q_rim, row_total, col_total)
    g_part = spread_tiles(g_rim, row_total, col_total)
    l_part = spread_tiles(log_rim, row_total, col_total)
    s_part = spread_tiles(spread_rim, row_total, col_total)
    scores = mix("hnkd,hnqd->hnkq", k_part, q_part) * score_scale
    soft_weights = jnp.where(inside[None, None], jnp.exp(scores - l_part[:, :, None, :]), 0.0)
    grad_probs = mix("hnkd,hnqd->hnkq", v_part, g_part)
    grad_scores = (soft_weights * (grad_probs - s_part[:, :, None, :]) * score_scale).astype(
        jnp.bfloat16
    )
    grad_keys = mix("hnkq,hnqd->hnkd", grad_scores, q_part)
    grad_values = mix("hnkq,hnqd->hnkd", soft_weights.astype(jnp.bfloat16), g_part)
    grad_pair = jnp.concatenate([grad_keys, grad_values]).astype(jnp.bfloat16)
    grad_pair = unpack_tiles(grad_pair, row_total, col_total)
    return grad_pair.reshape((2, head_count) + grad_pair.shape[1:])


def layer_norm(flat_rows):
    wide_values = flat_rows.astype(jnp.float32)
    center = jnp.mean(wide_values, axis=-1, keepdims=True)
    shifted = wide_values - center
    inverse = lax.rsqrt(jnp.mean(shifted * shifted, axis=-1, keepdims=True) + norm_eps)
    return (shifted * inverse, inverse)


def local(tokens, w_query, w_key, w_value, w_out, d_out):
    tile_rows, tile_cols, model_width = tokens.shape
    head_dim = model_width // HEADS
    token_count = tile_rows * tile_cols
    flat_rows = tokens.reshape(token_count, model_width)
    normed, inverse = layer_norm(flat_rows)
    hidden = normed.astype(jnp.bfloat16)

    def split_heads(weight):
        return weight.reshape(model_width, HEADS, head_dim)

    def project(weight):
        rows = mix("td,dhe->hte", hidden, split_heads(weight)).astype(jnp.bfloat16)
        return rows.reshape(HEADS, tile_rows, tile_cols, head_dim)

    q_heads = project(w_query)
    k_heads = project(w_key)
    v_heads = project(w_value)
    grad_flat = d_out.reshape(token_count, model_width)
    out_heads = w_out.reshape(HEADS, head_dim, model_width)
    g_heads = mix("tf,hef->hte", grad_flat, out_heads).astype(jnp.bfloat16)
    g_heads = g_heads.reshape(HEADS, tile_rows, tile_cols, head_dim)
    time_all = tile_rows * lax.axis_size(TIME_AXES)
    freq_all = tile_cols * lax.axis_size("freq")
    time_start = lax.axis_index(TIME_AXES) * tile_rows
    freq_start = lax.axis_index("freq") * tile_cols

    def inside_map(margin):
        time_pos = time_start - margin + jnp.arange(tile_rows + 2 * margin)
        freq_pos = freq_start - margin + jnp.arange(tile_cols + 2 * margin)
        time_ok = (time_pos >= 0) & (time_pos < time_all)
        freq_ok = (freq_pos >= 0) & (freq_pos < freq_all)
        return (time_ok[:, None] & freq_ok[None, :]).astype(jnp.float32)

    sides = ((TIME_AXES, 2), ("freq", 3))
    rim_all = extended(jnp.stack([k_heads, v_heads, q_heads, g_heads]), sides, window_reach)
    near_rim = rim_all[:2]
    beside_all = rim_all[2:]
    attended, grad_query, log_own, spread_own = attend_both(
        q_heads, near_rim[0], near_rim[1], g_heads, inside_map(window_reach), HEADS
    )
    stats_rim = extended(jnp.stack([log_own, spread_own]), sides, window_reach)
    grad_pair = attend_key_grad(
        k_heads, v_heads, beside_all[0], beside_all[1], stats_rim[0], stats_rim[1], HEADS
    ).reshape(2, HEADS, token_count, head_dim)
    grad_keys, grad_values = grad_pair[0], grad_pair[1]
    attended = attended.reshape(HEADS, token_count, head_dim)
    grad_query = grad_query.reshape(HEADS, token_count, head_dim)
    output = (flat_rows.astype(jnp.float32) + mix("hte,hef->tf", attended, out_heads)).astype(
        jnp.bfloat16
    )

    core = lax.axis_index("core")
    pair = [(0, 1), (1, 0)]
    hidden_split = hidden.reshape(token_count, HEADS, 2, head_dim // 2)
    attended_split = attended.reshape(HEADS, token_count, 2, head_dim // 2)
    hidden_mine = lax.dynamic_index_in_dim(hidden_split, core, axis=2, keepdims=False)
    hidden_theirs = lax.dynamic_index_in_dim(hidden_split, 1 - core, axis=2, keepdims=False)
    attended_mine = lax.dynamic_index_in_dim(attended_split, core, axis=2, keepdims=False)
    attended_theirs = lax.dynamic_index_in_dim(attended_split, 1 - core, axis=2, keepdims=False)
    hidden_got, attended_got, query_got, grad_got = lax.ppermute(
        (hidden_theirs, attended_theirs, grad_query, grad_flat), "core", pair
    )
    pair_got = lax.ppermute(grad_pair, "core", pair)
    keys_got, values_got = pair_got[0], pair_got[1]
    hidden_both = jnp.concatenate([hidden_mine, hidden_got], axis=0)
    attended_both = jnp.concatenate([attended_mine, attended_got], axis=1)
    grad_both = jnp.concatenate([grad_flat, grad_got], axis=0)
    half_rows = model_width // 2

    def weight_term(grad_heads, grad_heads_got):
        both = jnp.concatenate([grad_heads, grad_heads_got], axis=1)
        return mix("tab,hte->abhe", hidden_both, both).reshape(half_rows, model_width)

    term_rows = jnp.concatenate(
        [
            weight_term(grad_query, query_got),
            weight_term(grad_keys, keys_got),
            weight_term(grad_values, values_got),
            mix("atb,tf->abf", attended_both, grad_both).reshape(half_rows, model_width),
        ],
        axis=1,
    )
    summed = lax.psum(term_rows, ("tz", "freq"))
    row_count = model_width // (lax.axis_size(TIME_AXES) * lax.axis_size("freq"))
    row_start = (lax.axis_index("tz") * lax.axis_size("freq") + lax.axis_index("freq")) * row_count
    weight_grads = lax.dynamic_slice_in_dim(summed, row_start, row_count, axis=0).reshape(
        row_count, 4, model_width
    )
    grad_hidden = mix("hte,dhe->td", grad_query, split_heads(w_query))
    grad_hidden = grad_hidden + mix("hte,dhe->td", grad_keys, split_heads(w_key))
    grad_hidden = grad_hidden + mix("hte,dhe->td", grad_values, split_heads(w_value))
    center_grad = jnp.mean(grad_hidden, axis=-1, keepdims=True)
    along = jnp.mean(grad_hidden * normed, axis=-1, keepdims=True)
    input_grad = (
        grad_flat.astype(jnp.float32) + (grad_hidden - center_grad - normed * along) * inverse
    ).astype(jnp.bfloat16)
    return (
        output.reshape(tile_rows, tile_cols, model_width),
        input_grad.reshape(tile_rows, tile_cols, model_width),
        weight_grads,
    )


def solution(mesh):
    time_size, freq_size = mesh.shape["tm"], mesh.shape["freq"]
    inner = Mesh(mesh.devices.reshape(time_size // 2, 2, freq_size), ("tz", "core", "freq"))
    in_specs = (P(TIME_AXES, "freq", None), P(), P(), P(), P(), P(TIME_AXES, "freq", None))
    out_specs = (
        P(TIME_AXES, "freq", None),
        P(TIME_AXES, "freq", None),
        P(("tz", "core", "freq"), None, None),
    )
    return jax.shard_map(local, mesh=inner, in_specs=in_specs, out_specs=out_specs, check_vma=False)
```

```python
import math

import jax
import jax.numpy as jnp
from jax import lax
from jax.sharding import Mesh, PartitionSpec as P

HEADS = 8
TIME_AXES = ("tz", "core")


window_reach = 6
tile_edge = 8
span_edge = 20
norm_eps = 1e-05
far_value = -1e30


def extended(array, sides, width):
    for axis, dim in sides:
        size, length = (lax.axis_size(axis), array.shape[dim])
        up = [(i, (i + 1) % size) for i in range(size - 1)]
        down = [(j, i) for i, j in up]
        last = lax.slice_in_dim(array, length - width, length, axis=dim)
        leading = lax.slice_in_dim(array, 0, width, axis=dim)
        before = lax.ppermute(last, axis, up)
        after = lax.ppermute(leading, axis, down)
        array = jnp.concatenate([before, array, after], axis=dim)
    return array


def mix(form, left_operand, right_operand):
    return jnp.einsum(form, left_operand, right_operand, preferred_element_type=jnp.float32)


def window_mask():
    query_pos = jnp.arange(tile_edge * tile_edge)
    key_pos = jnp.arange(span_edge * span_edge)
    rise_rows = (key_pos // span_edge)[None, :] - (query_pos // tile_edge)[:, None]
    rise_cols = (key_pos % span_edge)[None, :] - (query_pos % tile_edge)[:, None]
    return (
        (rise_rows >= 0)
        & (rise_rows <= 2 * window_reach)
        & (rise_cols >= 0)
        & (rise_cols <= 2 * window_reach)
    )


def pack_tiles(field_map):
    lead, row_total, col_total = field_map.shape[:3]
    trailing = field_map.shape[3:]
    shaped = field_map.reshape(
        (lead, row_total // tile_edge, tile_edge, col_total // tile_edge, tile_edge) + trailing
    )
    axes_order = (0, 1, 3, 2, 4) + tuple(range(5, shaped.ndim))
    return shaped.transpose(axes_order).reshape(
        (lead, row_total // tile_edge * (col_total // tile_edge), tile_edge * tile_edge)
        + trailing
    )


def unpack_tiles(tile_stack, row_total, col_total):
    lead = tile_stack.shape[0]
    trailing = tile_stack.shape[3:]
    shaped = tile_stack.reshape(
        (lead, row_total // tile_edge, col_total // tile_edge, tile_edge, tile_edge) + trailing
    )
    axes_order = (0, 1, 3, 2, 4) + tuple(range(5, shaped.ndim))
    return shaped.transpose(axes_order).reshape((lead, row_total, col_total) + trailing)


def spread_tiles(field_map, row_total, col_total):
    lead = field_map.shape[0]
    trailing = field_map.shape[3:]
    spans = []
    for tile_row in range(row_total // tile_edge):
        for tile_col in range(col_total // tile_edge):
            row_at, col_at = tile_row * tile_edge, tile_col * tile_edge
            spans.append(
                field_map[:, row_at : row_at + span_edge, col_at : col_at + span_edge].reshape(
                    (lead, span_edge * span_edge) + trailing
                )
            )
    return jnp.stack(spans, axis=1)


def attend_both(q_heads, k_rim, v_rim, g_heads, key_ok, head_count):
    head_count, row_total, col_total, head_dim = q_heads.shape
    score_scale = 1.0 / math.sqrt(head_dim)
    inside = window_mask()
    q_part = pack_tiles(q_heads)
    g_part = pack_tiles(g_heads)
    k_part = spread_tiles(k_rim, row_total, col_total)
    v_part = spread_tiles(v_rim, row_total, col_total)
    ok_part = spread_tiles(key_ok[None], row_total, col_total)[0]
    allowed = inside[None, None] & (ok_part[None, :, None, :] > 0.5)
    scores = mix("hnqd,hnkd->hnqk", q_part, k_part) * score_scale
    scores = jnp.where(allowed, scores, far_value)
    row_max = jnp.max(scores, axis=-1, keepdims=True)
    log_total = row_max + jnp.log(jnp.sum(jnp.exp(scores - row_max), axis=-1, keepdims=True))
    soft_weights = jnp.where(allowed, jnp.exp(scores - log_total), 0.0)
    attended = mix("hnqk,hnkd->hnqd", soft_weights.astype(jnp.bfloat16), v_part)
    grad_probs = mix("hnqd,hnkd->hnqk", g_part, v_part)
    spread = jnp.sum(soft_weights * grad_probs, axis=-1, keepdims=True)
    grad_scores = (soft_weights * (grad_probs - spread) * score_scale).astype(jnp.bfloat16)
    grad_query = mix("hnqk,hnkd->hnqd", grad_scores, k_part)
    return (
        unpack_tiles(attended.astype(jnp.bfloat16), row_total, col_total),
        unpack_tiles(grad_query.astype(jnp.bfloat16), row_total, col_total),
        unpack_tiles(log_total[..., 0], row_total, col_total),
        unpack_tiles(spread[..., 0], row_total, col_total),
    )


def attend_key_grad(k_heads, v_heads, q_rim, g_rim, log_rim, spread_rim, head_count):
    head_count, row_total, col_total, head_dim = k_heads.shape
    score_scale = 1.0 / math.sqrt(head_dim)
    inside = window_mask()
    k_part = pack_tiles(k_heads)
    v_part = pack_tiles(v_heads)
    q_part = spread_tiles(q_rim, row_total, col_total)
    g_part = spread_tiles(g_rim, row_total, col_total)
    l_part = spread_tiles(log_rim, row_total, col_total)
    s_part = spread_tiles(spread_rim, row_total, col_total)
    scores = mix("hnkd,hnqd->hnkq", k_part, q_part) * score_scale
    soft_weights = jnp.where(inside[None, None], jnp.exp(scores - l_part[:, :, None, :]), 0.0)
    grad_probs = mix("hnkd,hnqd->hnkq", v_part, g_part)
    grad_scores = (soft_weights * (grad_probs - s_part[:, :, None, :]) * score_scale).astype(
        jnp.bfloat16
    )
    grad_keys = mix("hnkq,hnqd->hnkd", grad_scores, q_part)
    grad_values = mix("hnkq,hnqd->hnkd", soft_weights.astype(jnp.bfloat16), g_part)
    return (
        unpack_tiles(grad_keys.astype(jnp.bfloat16), row_total, col_total),
        unpack_tiles(grad_values.astype(jnp.bfloat16), row_total, col_total),
    )


def layer_norm(flat_rows):
    wide_values = flat_rows.astype(jnp.float32)
    center = jnp.mean(wide_values, axis=-1, keepdims=True)
    shifted = wide_values - center
    inverse = lax.rsqrt(jnp.mean(shifted * shifted, axis=-1, keepdims=True) + norm_eps)
    return (shifted * inverse, inverse)


def local(tokens, w_query, w_key, w_value, w_out, d_out):
    tile_rows, tile_cols, model_width = tokens.shape
    head_dim = model_width // HEADS
    token_count = tile_rows * tile_cols
    flat_rows = tokens.reshape(token_count, model_width)
    normed, inverse = layer_norm(flat_rows)
    hidden = normed.astype(jnp.bfloat16)

    def split_heads(weight):
        return weight.reshape(model_width, HEADS, head_dim)

    def project(weight):
        rows = mix("td,dhe->hte", hidden, split_heads(weight)).astype(jnp.bfloat16)
        return rows.reshape(HEADS, tile_rows, tile_cols, head_dim)

    q_heads = project(w_query)
    k_heads = project(w_key)
    v_heads = project(w_value)
    grad_flat = d_out.reshape(token_count, model_width)
    out_heads = w_out.reshape(HEADS, head_dim, model_width)
    g_heads = mix("tf,hef->hte", grad_flat, out_heads).astype(jnp.bfloat16)
    g_heads = g_heads.reshape(HEADS, tile_rows, tile_cols, head_dim)
    time_all = tile_rows * lax.axis_size(TIME_AXES)
    freq_all = tile_cols * lax.axis_size("freq")
    time_start = lax.axis_index(TIME_AXES) * tile_rows
    freq_start = lax.axis_index("freq") * tile_cols

    def inside_map(margin):
        time_pos = time_start - margin + jnp.arange(tile_rows + 2 * margin)
        freq_pos = freq_start - margin + jnp.arange(tile_cols + 2 * margin)
        time_ok = (time_pos >= 0) & (time_pos < time_all)
        freq_ok = (freq_pos >= 0) & (freq_pos < freq_all)
        return (time_ok[:, None] & freq_ok[None, :]).astype(jnp.float32)

    sides = ((TIME_AXES, 2), ("freq", 3))
    near_rim = extended(jnp.stack([k_heads, v_heads]), sides, window_reach)
    beside_all = extended(jnp.stack([q_heads, g_heads]), sides, window_reach)
    attended, grad_query, log_own, spread_own = attend_both(
        q_heads, near_rim[0], near_rim[1], g_heads, inside_map(window_reach), HEADS
    )
    stats_rim = extended(jnp.stack([log_own, spread_own]), sides, window_reach)
    grad_keys, grad_values = attend_key_grad(
        k_heads, v_heads, beside_all[0], beside_all[1], stats_rim[0], stats_rim[1], HEADS
    )
    attended = attended.reshape(HEADS, token_count, head_dim)
    grad_query = grad_query.reshape(HEADS, token_count, head_dim)
    grad_keys = grad_keys.reshape(HEADS, token_count, head_dim)
    grad_values = grad_values.reshape(HEADS, token_count, head_dim)
    output = (flat_rows.astype(jnp.float32) + mix("hte,hef->tf", attended, out_heads)).astype(
        jnp.bfloat16
    )

    core = lax.axis_index("core")
    pair = [(0, 1), (1, 0)]
    hidden_got, attended_got, query_got, keys_got, values_got, grad_got = lax.ppermute(
        (hidden, attended, grad_query, grad_keys, grad_values, grad_flat), "core", pair
    )
    hidden_both = jnp.concatenate([hidden, hidden_got], axis=0).reshape(
        2 * token_count, HEADS, 2, head_dim // 2
    )
    hidden_both = lax.dynamic_index_in_dim(hidden_both, core, axis=2, keepdims=False)
    attended_both = jnp.concatenate([attended, attended_got], axis=1).reshape(
        HEADS, 2 * token_count, 2, head_dim // 2
    )
    attended_both = lax.dynamic_index_in_dim(attended_both, core, axis=2, keepdims=False)
    grad_both = jnp.concatenate([grad_flat, grad_got], axis=0)
    half_rows = model_width // 2

    def weight_term(grad_heads, grad_heads_got):
        both = jnp.concatenate([grad_heads, grad_heads_got], axis=1)
        return mix("tab,hte->abhe", hidden_both, both).reshape(half_rows, model_width)

    term_rows = jnp.concatenate(
        [
            weight_term(grad_query, query_got),
            weight_term(grad_keys, keys_got),
            weight_term(grad_values, values_got),
            mix("atb,tf->abf", attended_both, grad_both).reshape(half_rows, model_width),
        ],
        axis=1,
    )
    summed = lax.psum(term_rows, ("tz", "freq"))
    row_count = model_width // (lax.axis_size(TIME_AXES) * lax.axis_size("freq"))
    row_start = (lax.axis_index("tz") * lax.axis_size("freq") + lax.axis_index("freq")) * row_count
    weight_grads = lax.dynamic_slice_in_dim(summed, row_start, row_count, axis=0).reshape(
        row_count, 4, model_width
    )
    grad_hidden = mix("hte,dhe->td", grad_query, split_heads(w_query))
    grad_hidden = grad_hidden + mix("hte,dhe->td", grad_keys, split_heads(w_key))
    grad_hidden = grad_hidden + mix("hte,dhe->td", grad_values, split_heads(w_value))
    center_grad = jnp.mean(grad_hidden, axis=-1, keepdims=True)
    along = jnp.mean(grad_hidden * normed, axis=-1, keepdims=True)
    input_grad = (
        grad_flat.astype(jnp.float32) + (grad_hidden - center_grad - normed * along) * inverse
    ).astype(jnp.bfloat16)
    return (
        output.reshape(tile_rows, tile_cols, model_width),
        input_grad.reshape(tile_rows, tile_cols, model_width),
        weight_grads,
    )


def solution(mesh):
    time_size, freq_size = mesh.shape["tm"], mesh.shape["freq"]
    inner = Mesh(mesh.devices.reshape(time_size // 2, 2, freq_size), ("tz", "core", "freq"))
    in_specs = (P(TIME_AXES, "freq", None), P(), P(), P(), P(), P(TIME_AXES, "freq", None))
    out_specs = (
        P(TIME_AXES, "freq", None),
        P(TIME_AXES, "freq", None),
        P(("tz", "core", "freq"), None, None),
    )
    return jax.shard_map(local, mesh=inner, in_specs=in_specs, out_specs=out_specs, check_vma=False)
```

```python
import math

import jax
import jax.numpy as jnp
from jax import lax
from jax.sharding import Mesh, PartitionSpec as P

HEADS = 8
TIME_AXES = ("tz", "core")


window_reach = 6
tile_edge = 8
span_edge = 20
norm_eps = 1e-05
far_value = -1e30


def extended(array, sides, width):
    for axis, dim in sides:
        size, length = (lax.axis_size(axis), array.shape[dim])
        up = [(i, (i + 1) % size) for i in range(size - 1)]
        down = [(j, i) for i, j in up]
        last = lax.slice_in_dim(array, length - width, length, axis=dim)
        leading = lax.slice_in_dim(array, 0, width, axis=dim)
        before = lax.ppermute(last, axis, up)
        after = lax.ppermute(leading, axis, down)
        array = jnp.concatenate([before, array, after], axis=dim)
    return array


def mix(form, left_operand, right_operand):
    return jnp.einsum(form, left_operand, right_operand, preferred_element_type=jnp.float32)


def window_mask():
    query_pos = jnp.arange(tile_edge * tile_edge)
    key_pos = jnp.arange(span_edge * span_edge)
    rise_rows = (key_pos // span_edge)[None, :] - (query_pos // tile_edge)[:, None]
    rise_cols = (key_pos % span_edge)[None, :] - (query_pos % tile_edge)[:, None]
    return (
        (rise_rows >= 0)
        & (rise_rows <= 2 * window_reach)
        & (rise_cols >= 0)
        & (rise_cols <= 2 * window_reach)
    )


def pack_tiles(field_map):
    lead, row_total, col_total = field_map.shape[:3]
    trailing = field_map.shape[3:]
    shaped = field_map.reshape(
        (lead, row_total // tile_edge, tile_edge, col_total // tile_edge, tile_edge) + trailing
    )
    axes_order = (0, 1, 3, 2, 4) + tuple(range(5, shaped.ndim))
    return shaped.transpose(axes_order).reshape(
        (lead, row_total // tile_edge * (col_total // tile_edge), tile_edge * tile_edge)
        + trailing
    )


def unpack_tiles(tile_stack, row_total, col_total):
    lead = tile_stack.shape[0]
    trailing = tile_stack.shape[3:]
    shaped = tile_stack.reshape(
        (lead, row_total // tile_edge, col_total // tile_edge, tile_edge, tile_edge) + trailing
    )
    axes_order = (0, 1, 3, 2, 4) + tuple(range(5, shaped.ndim))
    return shaped.transpose(axes_order).reshape((lead, row_total, col_total) + trailing)


def spread_tiles(field_map, row_total, col_total):
    lead = field_map.shape[0]
    trailing = field_map.shape[3:]
    spans = []
    for tile_row in range(row_total // tile_edge):
        for tile_col in range(col_total // tile_edge):
            row_at, col_at = tile_row * tile_edge, tile_col * tile_edge
            spans.append(
                field_map[:, row_at : row_at + span_edge, col_at : col_at + span_edge].reshape(
                    (lead, span_edge * span_edge) + trailing
                )
            )
    return jnp.stack(spans, axis=1)


def attend_both(q_heads, k_rim, v_rim, g_heads, key_ok, head_count):
    head_count, row_total, col_total, head_dim = q_heads.shape
    score_scale = 1.0 / math.sqrt(head_dim)
    inside = window_mask()
    q_part = pack_tiles(q_heads)
    g_part = pack_tiles(g_heads)
    k_part = spread_tiles(k_rim, row_total, col_total)
    v_part = spread_tiles(v_rim, row_total, col_total)
    ok_part = spread_tiles(key_ok[None], row_total, col_total)[0]
    allowed = inside[None, None] & (ok_part[None, :, None, :] > 0.5)
    scores = mix("hnqd,hnkd->hnqk", q_part, k_part) * score_scale
    scores = jnp.where(allowed, scores, far_value)
    row_max = jnp.max(scores, axis=-1, keepdims=True)
    log_total = row_max + jnp.log(jnp.sum(jnp.exp(scores - row_max), axis=-1, keepdims=True))
    soft_weights = jnp.where(allowed, jnp.exp(scores - log_total), 0.0)
    attended = mix("hnqk,hnkd->hnqd", soft_weights.astype(jnp.bfloat16), v_part)
    grad_probs = mix("hnqd,hnkd->hnqk", g_part, v_part)
    spread = jnp.sum(soft_weights * grad_probs, axis=-1, keepdims=True)
    grad_scores = (soft_weights * (grad_probs - spread) * score_scale).astype(jnp.bfloat16)
    grad_query = mix("hnqk,hnkd->hnqd", grad_scores, k_part)
    return (
        unpack_tiles(attended.astype(jnp.bfloat16), row_total, col_total),
        unpack_tiles(grad_query.astype(jnp.bfloat16), row_total, col_total),
        unpack_tiles(log_total[..., 0], row_total, col_total),
        unpack_tiles(spread[..., 0], row_total, col_total),
    )


def attend_key_grad(k_heads, v_heads, q_rim, g_rim, log_rim, spread_rim, head_count):
    head_count, row_total, col_total, head_dim = k_heads.shape
    score_scale = 1.0 / math.sqrt(head_dim)
    inside = window_mask()
    k_part = pack_tiles(k_heads)
    v_part = pack_tiles(v_heads)
    q_part = spread_tiles(q_rim, row_total, col_total)
    g_part = spread_tiles(g_rim, row_total, col_total)
    l_part = spread_tiles(log_rim, row_total, col_total)
    s_part = spread_tiles(spread_rim, row_total, col_total)
    scores = mix("hnkd,hnqd->hnkq", k_part, q_part) * score_scale
    soft_weights = jnp.where(inside[None, None], jnp.exp(scores - l_part[:, :, None, :]), 0.0)
    grad_probs = mix("hnkd,hnqd->hnkq", v_part, g_part)
    grad_scores = (soft_weights * (grad_probs - s_part[:, :, None, :]) * score_scale).astype(
        jnp.bfloat16
    )
    grad_keys = mix("hnkq,hnqd->hnkd", grad_scores, q_part)
    grad_values = mix("hnkq,hnqd->hnkd", soft_weights.astype(jnp.bfloat16), g_part)
    return (
        unpack_tiles(grad_keys.astype(jnp.bfloat16), row_total, col_total),
        unpack_tiles(grad_values.astype(jnp.bfloat16), row_total, col_total),
    )


def layer_norm(flat_rows):
    wide_values = flat_rows.astype(jnp.float32)
    center = jnp.mean(wide_values, axis=-1, keepdims=True)
    shifted = wide_values - center
    inverse = lax.rsqrt(jnp.mean(shifted * shifted, axis=-1, keepdims=True) + norm_eps)
    return (shifted * inverse, inverse)


def local(tokens, w_query, w_key, w_value, w_out, d_out):
    tile_rows, tile_cols, model_width = tokens.shape
    head_dim = model_width // HEADS
    token_count = tile_rows * tile_cols
    flat_rows = tokens.reshape(token_count, model_width)
    normed, inverse = layer_norm(flat_rows)
    hidden = normed.astype(jnp.bfloat16)

    def split_heads(weight):
        return weight.reshape(model_width, HEADS, head_dim)

    def project(weight):
        rows = mix("td,dhe->hte", hidden, split_heads(weight)).astype(jnp.bfloat16)
        return rows.reshape(HEADS, tile_rows, tile_cols, head_dim)

    q_heads = project(w_query)
    k_heads = project(w_key)
    v_heads = project(w_value)
    grad_flat = d_out.reshape(token_count, model_width)
    out_heads = w_out.reshape(HEADS, head_dim, model_width)
    g_heads = mix("tf,hef->hte", grad_flat, out_heads).astype(jnp.bfloat16)
    g_heads = g_heads.reshape(HEADS, tile_rows, tile_cols, head_dim)
    time_all = tile_rows * lax.axis_size(TIME_AXES)
    freq_all = tile_cols * lax.axis_size("freq")
    time_start = lax.axis_index(TIME_AXES) * tile_rows
    freq_start = lax.axis_index("freq") * tile_cols

    def inside_map(margin):
        time_pos = time_start - margin + jnp.arange(tile_rows + 2 * margin)
        freq_pos = freq_start - margin + jnp.arange(tile_cols + 2 * margin)
        time_ok = (time_pos >= 0) & (time_pos < time_all)
        freq_ok = (freq_pos >= 0) & (freq_pos < freq_all)
        return (time_ok[:, None] & freq_ok[None, :]).astype(jnp.float32)

    sides = ((TIME_AXES, 2), ("freq", 3))
    near_rim = extended(jnp.stack([k_heads, v_heads]), sides, window_reach)
    beside_all = extended(jnp.stack([q_heads, g_heads]), sides, window_reach)
    attended, grad_query, log_own, spread_own = attend_both(
        q_heads, near_rim[0], near_rim[1], g_heads, inside_map(window_reach), HEADS
    )
    stats_rim = extended(jnp.stack([log_own, spread_own]), sides, window_reach)
    grad_keys, grad_values = attend_key_grad(
        k_heads, v_heads, beside_all[0], beside_all[1], stats_rim[0], stats_rim[1], HEADS
    )
    attended = attended.reshape(HEADS, token_count, head_dim)
    grad_query = grad_query.reshape(HEADS, token_count, head_dim)
    grad_keys = grad_keys.reshape(HEADS, token_count, head_dim)
    grad_values = grad_values.reshape(HEADS, token_count, head_dim)
    output = (flat_rows.astype(jnp.float32) + mix("hte,hef->tf", attended, out_heads)).astype(
        jnp.bfloat16
    )

    core = lax.axis_index("core")
    pair = [(0, 1), (1, 0)]
    hidden_split = hidden.reshape(token_count, HEADS, 2, head_dim // 2)
    attended_split = attended.reshape(HEADS, token_count, 2, head_dim // 2)
    hidden_mine = lax.dynamic_index_in_dim(hidden_split, core, axis=2, keepdims=False)
    hidden_theirs = lax.dynamic_index_in_dim(hidden_split, 1 - core, axis=2, keepdims=False)
    attended_mine = lax.dynamic_index_in_dim(attended_split, core, axis=2, keepdims=False)
    attended_theirs = lax.dynamic_index_in_dim(attended_split, 1 - core, axis=2, keepdims=False)
    hidden_got, attended_got, query_got, keys_got, values_got, grad_got = lax.ppermute(
        (hidden_theirs, attended_theirs, grad_query, grad_keys, grad_values, grad_flat),
        "core",
        pair,
    )
    hidden_both = jnp.concatenate([hidden_mine, hidden_got], axis=0)
    attended_both = jnp.concatenate([attended_mine, attended_got], axis=1)
    grad_both = jnp.concatenate([grad_flat, grad_got], axis=0)
    half_rows = model_width // 2

    def weight_term(grad_heads, grad_heads_got):
        both = jnp.concatenate([grad_heads, grad_heads_got], axis=1)
        return mix("tab,hte->abhe", hidden_both, both).reshape(half_rows, model_width)

    terms = (
        weight_term(grad_query, query_got),
        weight_term(grad_keys, keys_got),
        weight_term(grad_values, values_got),
        mix("atb,tf->abf", attended_both, grad_both).reshape(half_rows, model_width),
    )
    summed = lax.psum(terms, ("tz", "freq"))
    row_count = model_width // (lax.axis_size(TIME_AXES) * lax.axis_size("freq"))
    row_start = (lax.axis_index("tz") * lax.axis_size("freq") + lax.axis_index("freq")) * row_count
    weight_grads = jnp.stack(
        [lax.dynamic_slice_in_dim(part, row_start, row_count, axis=0) for part in summed], axis=1
    )
    grad_hidden = mix("hte,dhe->td", grad_query, split_heads(w_query))
    grad_hidden = grad_hidden + mix("hte,dhe->td", grad_keys, split_heads(w_key))
    grad_hidden = grad_hidden + mix("hte,dhe->td", grad_values, split_heads(w_value))
    center_grad = jnp.mean(grad_hidden, axis=-1, keepdims=True)
    along = jnp.mean(grad_hidden * normed, axis=-1, keepdims=True)
    input_grad = (
        grad_flat.astype(jnp.float32) + (grad_hidden - center_grad - normed * along) * inverse
    ).astype(jnp.bfloat16)
    return (
        output.reshape(tile_rows, tile_cols, model_width),
        input_grad.reshape(tile_rows, tile_cols, model_width),
        weight_grads,
    )


def solution(mesh):
    time_size, freq_size = mesh.shape["tm"], mesh.shape["freq"]
    inner = Mesh(mesh.devices.reshape(time_size // 2, 2, freq_size), ("tz", "core", "freq"))
    in_specs = (P(TIME_AXES, "freq", None), P(), P(), P(), P(), P(TIME_AXES, "freq", None))
    out_specs = (
        P(TIME_AXES, "freq", None),
        P(TIME_AXES, "freq", None),
        P(("tz", "core", "freq"), None, None),
    )
    return jax.shard_map(local, mesh=inner, in_specs=in_specs, out_specs=out_specs, check_vma=False)
```

```python
import math

import jax
import jax.numpy as jnp
from jax import lax
from jax.sharding import Mesh, PartitionSpec as P

HEADS = 8
TIME_AXES = ("tz", "core")


window_reach = 6
tile_edge = 8
span_edge = 20
norm_eps = 1e-05
far_value = -1e30


def extended(array, sides, width):
    for axis, dim in sides:
        size, length = (lax.axis_size(axis), array.shape[dim])
        up = [(i, (i + 1) % size) for i in range(size - 1)]
        down = [(j, i) for i, j in up]
        last = lax.slice_in_dim(array, length - width, length, axis=dim)
        leading = lax.slice_in_dim(array, 0, width, axis=dim)
        before = lax.ppermute(last, axis, up)
        after = lax.ppermute(leading, axis, down)
        array = jnp.concatenate([before, array, after], axis=dim)
    return array


def folded(array, sides, width):
    for axis, dim in reversed(sides):
        size, length = (lax.axis_size(axis), array.shape[dim])
        up = [(i, (i + 1) % size) for i in range(size - 1)]
        down = [(j, i) for i, j in up]
        before = lax.slice_in_dim(array, 0, width, axis=dim)
        after = lax.slice_in_dim(array, length - width, length, axis=dim)
        own = lax.slice_in_dim(array, width, length - width, axis=dim)
        from_next = lax.ppermute(before, axis, down)
        from_prior = lax.ppermute(after, axis, up)
        inner = own.shape[dim]
        own = own + jnp.concatenate(
            [
                from_prior,
                jnp.zeros_like(lax.slice_in_dim(own, 0, inner - 2 * width, axis=dim)),
                from_next,
            ],
            axis=dim,
        )
        array = own
    return array


def mix(form, left_operand, right_operand):
    return jnp.einsum(form, left_operand, right_operand, preferred_element_type=jnp.float32)


def window_mask():
    query_pos = jnp.arange(tile_edge * tile_edge)
    key_pos = jnp.arange(span_edge * span_edge)
    rise_rows = (key_pos // span_edge)[None, :] - (query_pos // tile_edge)[:, None]
    rise_cols = (key_pos % span_edge)[None, :] - (query_pos % tile_edge)[:, None]
    return (
        (rise_rows >= 0)
        & (rise_rows <= 2 * window_reach)
        & (rise_cols >= 0)
        & (rise_cols <= 2 * window_reach)
    )


def pack_tiles(field_map):
    lead, row_total, col_total = field_map.shape[:3]
    trailing = field_map.shape[3:]
    shaped = field_map.reshape(
        (lead, row_total // tile_edge, tile_edge, col_total // tile_edge, tile_edge) + trailing
    )
    axes_order = (0, 1, 3, 2, 4) + tuple(range(5, shaped.ndim))
    return shaped.transpose(axes_order).reshape(
        (lead, row_total // tile_edge * (col_total // tile_edge), tile_edge * tile_edge)
        + trailing
    )


def unpack_tiles(tile_stack, row_total, col_total):
    lead = tile_stack.shape[0]
    trailing = tile_stack.shape[3:]
    shaped = tile_stack.reshape(
        (lead, row_total // tile_edge, col_total // tile_edge, tile_edge, tile_edge) + trailing
    )
    axes_order = (0, 1, 3, 2, 4) + tuple(range(5, shaped.ndim))
    return shaped.transpose(axes_order).reshape((lead, row_total, col_total) + trailing)


def spread_tiles(field_map, row_total, col_total):
    lead = field_map.shape[0]
    trailing = field_map.shape[3:]
    spans = []
    for tile_row in range(row_total // tile_edge):
        for tile_col in range(col_total // tile_edge):
            row_at, col_at = tile_row * tile_edge, tile_col * tile_edge
            spans.append(
                field_map[:, row_at : row_at + span_edge, col_at : col_at + span_edge].reshape(
                    (lead, span_edge * span_edge) + trailing
                )
            )
    return jnp.stack(spans, axis=1)


def attend_both(q_heads, k_rim, v_rim, g_heads, key_ok, head_count):
    head_count, row_total, col_total, head_dim = q_heads.shape
    score_scale = 1.0 / math.sqrt(head_dim)
    inside = window_mask()
    q_part = pack_tiles(q_heads)
    g_part = pack_tiles(g_heads)
    k_part = spread_tiles(k_rim, row_total, col_total)
    v_part = spread_tiles(v_rim, row_total, col_total)
    ok_part = spread_tiles(key_ok[None], row_total, col_total)[0]
    allowed = inside[None, None] & (ok_part[None, :, None, :] > 0.5)
    scores = mix("hnqd,hnkd->hnqk", q_part, k_part) * score_scale
    scores = jnp.where(allowed, scores, far_value)
    row_max = jnp.max(scores, axis=-1, keepdims=True)
    log_total = row_max + jnp.log(jnp.sum(jnp.exp(scores - row_max), axis=-1, keepdims=True))
    soft_weights = jnp.where(allowed, jnp.exp(scores - log_total), 0.0)
    attended = mix("hnqk,hnkd->hnqd", soft_weights.astype(jnp.bfloat16), v_part)
    grad_probs = mix("hnqd,hnkd->hnqk", g_part, v_part)
    spread = jnp.sum(soft_weights * grad_probs, axis=-1, keepdims=True)
    grad_scores = (soft_weights * (grad_probs - spread) * score_scale).astype(jnp.bfloat16)
    grad_query = mix("hnqk,hnkd->hnqd", grad_scores, k_part)
    key_spans = mix("hnqk,hnqd->hnkd", grad_scores, q_part)
    value_spans = mix("hnqk,hnqd->hnkd", soft_weights.astype(jnp.bfloat16), g_part)
    span_pair = jnp.stack([key_spans, value_spans])
    rim_shape = (2, head_count, row_total + 2 * window_reach, col_total + 2 * window_reach, head_dim)
    rim = jnp.zeros(rim_shape, jnp.float32)
    tile_index = 0
    for tile_row in range(row_total // tile_edge):
        for tile_col in range(col_total // tile_edge):
            row_at, col_at = tile_row * tile_edge, tile_col * tile_edge
            piece = span_pair[:, :, tile_index].reshape(
                (2, head_count, span_edge, span_edge, head_dim)
            )
            rim = rim.at[:, :, row_at : row_at + span_edge, col_at : col_at + span_edge].add(piece)
            tile_index += 1
    return (
        rim,
        unpack_tiles(attended.astype(jnp.bfloat16), row_total, col_total),
        unpack_tiles(grad_query.astype(jnp.bfloat16), row_total, col_total),
        unpack_tiles(log_total[..., 0], row_total, col_total),
        unpack_tiles(spread[..., 0], row_total, col_total),
    )


def attend_key_grad(k_heads, v_heads, q_rim, g_rim, log_rim, spread_rim, head_count):
    head_count, row_total, col_total, head_dim = k_heads.shape
    score_scale = 1.0 / math.sqrt(head_dim)
    inside = window_mask()
    k_part = pack_tiles(k_heads)
    v_part = pack_tiles(v_heads)
    q_part = spread_tiles(q_rim, row_total, col_total)
    g_part = spread_tiles(g_rim, row_total, col_total)
    l_part = spread_tiles(log_rim, row_total, col_total)
    s_part = spread_tiles(spread_rim, row_total, col_total)
    scores = mix("hnkd,hnqd->hnkq", k_part, q_part) * score_scale
    soft_weights = jnp.where(inside[None, None], jnp.exp(scores - l_part[:, :, None, :]), 0.0)
    grad_probs = mix("hnkd,hnqd->hnkq", v_part, g_part)
    grad_scores = (soft_weights * (grad_probs - s_part[:, :, None, :]) * score_scale).astype(
        jnp.bfloat16
    )
    grad_keys = mix("hnkq,hnqd->hnkd", grad_scores, q_part)
    grad_values = mix("hnkq,hnqd->hnkd", soft_weights.astype(jnp.bfloat16), g_part)
    return (
        unpack_tiles(grad_keys.astype(jnp.bfloat16), row_total, col_total),
        unpack_tiles(grad_values.astype(jnp.bfloat16), row_total, col_total),
    )


def layer_norm(flat_rows):
    wide_values = flat_rows.astype(jnp.float32)
    center = jnp.mean(wide_values, axis=-1, keepdims=True)
    shifted = wide_values - center
    inverse = lax.rsqrt(jnp.mean(shifted * shifted, axis=-1, keepdims=True) + norm_eps)
    return (shifted * inverse, inverse)


def local(tokens, w_query, w_key, w_value, w_out, d_out):
    tile_rows, tile_cols, model_width = tokens.shape
    head_dim = model_width // HEADS
    token_count = tile_rows * tile_cols
    flat_rows = tokens.reshape(token_count, model_width)
    normed, inverse = layer_norm(flat_rows)
    hidden = normed.astype(jnp.bfloat16)

    def split_heads(weight):
        return weight.reshape(model_width, HEADS, head_dim)

    def project(weight):
        rows = mix("td,dhe->hte", hidden, split_heads(weight)).astype(jnp.bfloat16)
        return rows.reshape(HEADS, tile_rows, tile_cols, head_dim)

    q_heads = project(w_query)
    k_heads = project(w_key)
    v_heads = project(w_value)
    grad_flat = d_out.reshape(token_count, model_width)
    out_heads = w_out.reshape(HEADS, head_dim, model_width)
    g_heads = mix("tf,hef->hte", grad_flat, out_heads).astype(jnp.bfloat16)
    g_heads = g_heads.reshape(HEADS, tile_rows, tile_cols, head_dim)
    time_all = tile_rows * lax.axis_size(TIME_AXES)
    freq_all = tile_cols * lax.axis_size("freq")
    time_start = lax.axis_index(TIME_AXES) * tile_rows
    freq_start = lax.axis_index("freq") * tile_cols

    def inside_map(margin):
        time_pos = time_start - margin + jnp.arange(tile_rows + 2 * margin)
        freq_pos = freq_start - margin + jnp.arange(tile_cols + 2 * margin)
        time_ok = (time_pos >= 0) & (time_pos < time_all)
        freq_ok = (freq_pos >= 0) & (freq_pos < freq_all)
        return (time_ok[:, None] & freq_ok[None, :]).astype(jnp.float32)

    sides = ((TIME_AXES, 2), ("freq", 3))
    near_rim = extended(jnp.stack([k_heads, v_heads]), sides, window_reach)
    grad_rim, attended, grad_query, log_own, spread_own = attend_both(
        q_heads, near_rim[0], near_rim[1], g_heads, inside_map(window_reach), HEADS
    )
    grad_pair = folded(grad_rim, sides, window_reach).astype(jnp.bfloat16)
    grad_keys = grad_pair[0]
    grad_values = grad_pair[1]
    attended = attended.reshape(HEADS, token_count, head_dim)
    grad_query = grad_query.reshape(HEADS, token_count, head_dim)
    grad_keys = grad_keys.reshape(HEADS, token_count, head_dim)
    grad_values = grad_values.reshape(HEADS, token_count, head_dim)
    output = (flat_rows.astype(jnp.float32) + mix("hte,hef->tf", attended, out_heads)).astype(
        jnp.bfloat16
    )

    core = lax.axis_index("core")
    pair = [(0, 1), (1, 0)]
    hidden_split = hidden.reshape(token_count, HEADS, 2, head_dim // 2)
    attended_split = attended.reshape(HEADS, token_count, 2, head_dim // 2)
    hidden_mine = lax.dynamic_index_in_dim(hidden_split, core, axis=2, keepdims=False)
    hidden_theirs = lax.dynamic_index_in_dim(hidden_split, 1 - core, axis=2, keepdims=False)
    attended_mine = lax.dynamic_index_in_dim(attended_split, core, axis=2, keepdims=False)
    attended_theirs = lax.dynamic_index_in_dim(attended_split, 1 - core, axis=2, keepdims=False)
    hidden_got, attended_got, query_got, keys_got, values_got, grad_got = lax.ppermute(
        (hidden_theirs, attended_theirs, grad_query, grad_keys, grad_values, grad_flat),
        "core",
        pair,
    )
    hidden_both = jnp.concatenate([hidden_mine, hidden_got], axis=0)
    attended_both = jnp.concatenate([attended_mine, attended_got], axis=1)
    grad_both = jnp.concatenate([grad_flat, grad_got], axis=0)
    half_rows = model_width // 2

    def weight_term(grad_heads, grad_heads_got):
        both = jnp.concatenate([grad_heads, grad_heads_got], axis=1)
        return mix("tab,hte->abhe", hidden_both, both).reshape(half_rows, model_width)

    term_rows = jnp.concatenate(
        [
            weight_term(grad_query, query_got),
            weight_term(grad_keys, keys_got),
            weight_term(grad_values, values_got),
            mix("atb,tf->abf", attended_both, grad_both).reshape(half_rows, model_width),
        ],
        axis=1,
    )
    summed = lax.psum(term_rows, ("tz", "freq"))
    row_count = model_width // (lax.axis_size(TIME_AXES) * lax.axis_size("freq"))
    row_start = (lax.axis_index("tz") * lax.axis_size("freq") + lax.axis_index("freq")) * row_count
    weight_grads = lax.dynamic_slice_in_dim(summed, row_start, row_count, axis=0).reshape(
        row_count, 4, model_width
    )
    grad_hidden = mix("hte,dhe->td", grad_query, split_heads(w_query))
    grad_hidden = grad_hidden + mix("hte,dhe->td", grad_keys, split_heads(w_key))
    grad_hidden = grad_hidden + mix("hte,dhe->td", grad_values, split_heads(w_value))
    center_grad = jnp.mean(grad_hidden, axis=-1, keepdims=True)
    along = jnp.mean(grad_hidden * normed, axis=-1, keepdims=True)
    input_grad = (
        grad_flat.astype(jnp.float32) + (grad_hidden - center_grad - normed * along) * inverse
    ).astype(jnp.bfloat16)
    return (
        output.reshape(tile_rows, tile_cols, model_width),
        input_grad.reshape(tile_rows, tile_cols, model_width),
        weight_grads,
    )


def solution(mesh):
    time_size, freq_size = mesh.shape["tm"], mesh.shape["freq"]
    inner = Mesh(mesh.devices.reshape(time_size // 2, 2, freq_size), ("tz", "core", "freq"))
    in_specs = (P(TIME_AXES, "freq", None), P(), P(), P(), P(), P(TIME_AXES, "freq", None))
    out_specs = (
        P(TIME_AXES, "freq", None),
        P(TIME_AXES, "freq", None),
        P(("tz", "core", "freq"), None, None),
    )
    return jax.shard_map(local, mesh=inner, in_specs=in_specs, out_specs=out_specs, check_vma=False)
```

```python
import math

import jax
import jax.numpy as jnp
from jax import lax
from jax.sharding import Mesh, PartitionSpec as P

HEADS = 8
TIME_AXES = ("tz", "core")


window_reach = 6
tile_edge = 8
span_edge = 20
norm_eps = 1e-05
far_value = -1e30


def extended(array, sides, width):
    for axis, dim in sides:
        size, length = (lax.axis_size(axis), array.shape[dim])
        up = [(i, (i + 1) % size) for i in range(size - 1)]
        down = [(j, i) for i, j in up]
        last = lax.slice_in_dim(array, length - width, length, axis=dim)
        leading = lax.slice_in_dim(array, 0, width, axis=dim)
        before = lax.ppermute(last, axis, up)
        after = lax.ppermute(leading, axis, down)
        array = jnp.concatenate([before, array, after], axis=dim)
    return array


def mix(form, left_operand, right_operand):
    return jnp.einsum(form, left_operand, right_operand, preferred_element_type=jnp.float32)


def window_mask():
    query_pos = jnp.arange(tile_edge * tile_edge)
    key_pos = jnp.arange(span_edge * span_edge)
    rise_rows = (key_pos // span_edge)[None, :] - (query_pos // tile_edge)[:, None]
    rise_cols = (key_pos % span_edge)[None, :] - (query_pos % tile_edge)[:, None]
    return (
        (rise_rows >= 0)
        & (rise_rows <= 2 * window_reach)
        & (rise_cols >= 0)
        & (rise_cols <= 2 * window_reach)
    )


def pack_tiles(field_map):
    lead, row_total, col_total = field_map.shape[:3]
    trailing = field_map.shape[3:]
    shaped = field_map.reshape(
        (lead, row_total // tile_edge, tile_edge, col_total // tile_edge, tile_edge) + trailing
    )
    axes_order = (0, 1, 3, 2, 4) + tuple(range(5, shaped.ndim))
    return shaped.transpose(axes_order).reshape(
        (lead, row_total // tile_edge * (col_total // tile_edge), tile_edge * tile_edge)
        + trailing
    )


def unpack_tiles(tile_stack, row_total, col_total):
    lead = tile_stack.shape[0]
    trailing = tile_stack.shape[3:]
    shaped = tile_stack.reshape(
        (lead, row_total // tile_edge, col_total // tile_edge, tile_edge, tile_edge) + trailing
    )
    axes_order = (0, 1, 3, 2, 4) + tuple(range(5, shaped.ndim))
    return shaped.transpose(axes_order).reshape((lead, row_total, col_total) + trailing)


def spread_tiles(field_map, row_total, col_total):
    lead = field_map.shape[0]
    trailing = field_map.shape[3:]
    spans = []
    for tile_row in range(row_total // tile_edge):
        for tile_col in range(col_total // tile_edge):
            row_at, col_at = tile_row * tile_edge, tile_col * tile_edge
            spans.append(
                field_map[:, row_at : row_at + span_edge, col_at : col_at + span_edge].reshape(
                    (lead, span_edge * span_edge) + trailing
                )
            )
    return jnp.stack(spans, axis=1)


def attend_both(q_heads, k_rim, v_rim, g_heads, key_ok, head_count):
    head_count, row_total, col_total, head_dim = q_heads.shape
    score_scale = 1.0 / math.sqrt(head_dim)
    inside = window_mask()
    q_part = pack_tiles(q_heads)
    g_part = pack_tiles(g_heads)
    k_part = spread_tiles(k_rim, row_total, col_total)
    v_part = spread_tiles(v_rim, row_total, col_total)
    ok_part = spread_tiles(key_ok[None], row_total, col_total)[0]
    allowed = inside[None, None] & (ok_part[None, :, None, :] > 0.5)
    scores = mix("hnqd,hnkd->hnqk", q_part, k_part) * score_scale
    scores = jnp.where(allowed, scores, far_value)
    row_max = jnp.max(scores, axis=-1, keepdims=True)
    log_total = row_max + jnp.log(jnp.sum(jnp.exp(scores - row_max), axis=-1, keepdims=True))
    soft_weights = jnp.where(allowed, jnp.exp(scores - log_total), 0.0)
    attended = mix("hnqk,hnkd->hnqd", soft_weights.astype(jnp.bfloat16), v_part)
    grad_probs = mix("hnqd,hnkd->hnqk", g_part, v_part)
    spread = jnp.sum(soft_weights * grad_probs, axis=-1, keepdims=True)
    grad_scores = (soft_weights * (grad_probs - spread) * score_scale).astype(jnp.bfloat16)
    grad_query = mix("hnqk,hnkd->hnqd", grad_scores, k_part)
    return (
        unpack_tiles(attended.astype(jnp.bfloat16), row_total, col_total),
        unpack_tiles(grad_query.astype(jnp.bfloat16), row_total, col_total),
        unpack_tiles(log_total[..., 0], row_total, col_total),
        unpack_tiles(spread[..., 0], row_total, col_total),
    )


def attend_key_grad(k_heads, v_heads, q_rim, g_rim, log_rim, spread_rim, head_count):
    head_count, row_total, col_total, head_dim = k_heads.shape
    score_scale = 1.0 / math.sqrt(head_dim)
    inside = window_mask()
    k_part = pack_tiles(k_heads)
    v_part = pack_tiles(v_heads)
    q_part = spread_tiles(q_rim, row_total, col_total)
    g_part = spread_tiles(g_rim, row_total, col_total)
    l_part = spread_tiles(log_rim, row_total, col_total)
    s_part = spread_tiles(spread_rim, row_total, col_total)
    scores = mix("hnkd,hnqd->hnkq", k_part, q_part) * score_scale
    soft_weights = jnp.where(inside[None, None], jnp.exp(scores - l_part[:, :, None, :]), 0.0)
    grad_probs = mix("hnkd,hnqd->hnkq", v_part, g_part)
    grad_scores = (soft_weights * (grad_probs - s_part[:, :, None, :]) * score_scale).astype(
        jnp.bfloat16
    )
    grad_keys = mix("hnkq,hnqd->hnkd", grad_scores, q_part)
    grad_values = mix("hnkq,hnqd->hnkd", soft_weights.astype(jnp.bfloat16), g_part)
    return (
        unpack_tiles(grad_keys.astype(jnp.bfloat16), row_total, col_total),
        unpack_tiles(grad_values.astype(jnp.bfloat16), row_total, col_total),
    )


def layer_norm(flat_rows):
    wide_values = flat_rows.astype(jnp.float32)
    center = jnp.mean(wide_values, axis=-1, keepdims=True)
    shifted = wide_values - center
    inverse = lax.rsqrt(jnp.mean(shifted * shifted, axis=-1, keepdims=True) + norm_eps)
    return (shifted * inverse, inverse)


def local(tokens, w_query, w_key, w_value, w_out, d_out):
    tile_rows, tile_cols, model_width = tokens.shape
    head_dim = model_width // HEADS
    token_count = tile_rows * tile_cols
    flat_rows = tokens.reshape(token_count, model_width)
    normed, inverse = layer_norm(flat_rows)
    hidden = normed.astype(jnp.bfloat16)

    def split_heads(weight):
        return weight.reshape(model_width, HEADS, head_dim)

    def project(weight):
        rows = mix("td,dhe->hte", hidden, split_heads(weight)).astype(jnp.bfloat16)
        return rows.reshape(HEADS, tile_rows, tile_cols, head_dim)

    q_heads = project(w_query)
    k_heads = project(w_key)
    v_heads = project(w_value)
    grad_flat = d_out.reshape(token_count, model_width)
    out_heads = w_out.reshape(HEADS, head_dim, model_width)
    g_heads = mix("tf,hef->hte", grad_flat, out_heads).astype(jnp.bfloat16)
    g_heads = g_heads.reshape(HEADS, tile_rows, tile_cols, head_dim)
    time_all = tile_rows * lax.axis_size(TIME_AXES)
    freq_all = tile_cols * lax.axis_size("freq")
    time_start = lax.axis_index(TIME_AXES) * tile_rows
    freq_start = lax.axis_index("freq") * tile_cols

    def inside_map(margin):
        time_pos = time_start - margin + jnp.arange(tile_rows + 2 * margin)
        freq_pos = freq_start - margin + jnp.arange(tile_cols + 2 * margin)
        time_ok = (time_pos >= 0) & (time_pos < time_all)
        freq_ok = (freq_pos >= 0) & (freq_pos < freq_all)
        return (time_ok[:, None] & freq_ok[None, :]).astype(jnp.float32)

    sides = ((TIME_AXES, 2), ("freq", 3))
    near_rim = extended(jnp.stack([k_heads, v_heads]), sides, window_reach)
    beside_all = extended(jnp.stack([q_heads, g_heads]), sides, window_reach)
    attended, grad_query, log_own, spread_own = attend_both(
        q_heads, near_rim[0], near_rim[1], g_heads, inside_map(window_reach), HEADS
    )
    stats_rim = extended(jnp.stack([log_own, spread_own]), sides, window_reach)
    grad_keys, grad_values = attend_key_grad(
        k_heads, v_heads, beside_all[0], beside_all[1], stats_rim[0], stats_rim[1], HEADS
    )
    attended = attended.reshape(HEADS, token_count, head_dim)
    grad_query = grad_query.reshape(HEADS, token_count, head_dim)
    grad_keys = grad_keys.reshape(HEADS, token_count, head_dim)
    grad_values = grad_values.reshape(HEADS, token_count, head_dim)
    output = (flat_rows.astype(jnp.float32) + mix("hte,hef->tf", attended, out_heads)).astype(
        jnp.bfloat16
    )

    core = lax.axis_index("core")
    pair = [(0, 1), (1, 0)]
    hidden_split = hidden.reshape(token_count, HEADS, 2, head_dim // 2)
    attended_split = attended.reshape(HEADS, token_count, 2, head_dim // 2)
    first_core = core == 0
    hidden_mine = jnp.where(first_core, hidden_split[:, :, 0], hidden_split[:, :, 1])
    hidden_theirs = jnp.where(first_core, hidden_split[:, :, 1], hidden_split[:, :, 0])
    attended_mine = jnp.where(first_core, attended_split[:, :, 0], attended_split[:, :, 1])
    attended_theirs = jnp.where(first_core, attended_split[:, :, 1], attended_split[:, :, 0])
    hidden_got, attended_got, query_got, keys_got, values_got, grad_got = lax.ppermute(
        (hidden_theirs, attended_theirs, grad_query, grad_keys, grad_values, grad_flat),
        "core",
        pair,
    )
    hidden_both = jnp.concatenate([hidden_mine, hidden_got], axis=0)
    attended_both = jnp.concatenate([attended_mine, attended_got], axis=1)
    grad_both = jnp.concatenate([grad_flat, grad_got], axis=0)
    half_rows = model_width // 2

    def weight_term(grad_heads, grad_heads_got):
        both = jnp.concatenate([grad_heads, grad_heads_got], axis=1)
        return mix("tab,hte->abhe", hidden_both, both).reshape(half_rows, model_width)

    term_rows = jnp.concatenate(
        [
            weight_term(grad_query, query_got),
            weight_term(grad_keys, keys_got),
            weight_term(grad_values, values_got),
            mix("atb,tf->abf", attended_both, grad_both).reshape(half_rows, model_width),
        ],
        axis=1,
    )
    summed = lax.psum(term_rows, ("tz", "freq"))
    row_count = model_width // (lax.axis_size(TIME_AXES) * lax.axis_size("freq"))
    row_start = (lax.axis_index("tz") * lax.axis_size("freq") + lax.axis_index("freq")) * row_count
    weight_grads = lax.dynamic_slice_in_dim(summed, row_start, row_count, axis=0).reshape(
        row_count, 4, model_width
    )
    grad_hidden = mix("hte,dhe->td", grad_query, split_heads(w_query))
    grad_hidden = grad_hidden + mix("hte,dhe->td", grad_keys, split_heads(w_key))
    grad_hidden = grad_hidden + mix("hte,dhe->td", grad_values, split_heads(w_value))
    center_grad = jnp.mean(grad_hidden, axis=-1, keepdims=True)
    along = jnp.mean(grad_hidden * normed, axis=-1, keepdims=True)
    input_grad = (
        grad_flat.astype(jnp.float32) + (grad_hidden - center_grad - normed * along) * inverse
    ).astype(jnp.bfloat16)
    return (
        output.reshape(tile_rows, tile_cols, model_width),
        input_grad.reshape(tile_rows, tile_cols, model_width),
        weight_grads,
    )


def solution(mesh):
    time_size, freq_size = mesh.shape["tm"], mesh.shape["freq"]
    inner = Mesh(mesh.devices.reshape(time_size // 2, 2, freq_size), ("tz", "core", "freq"))
    in_specs = (P(TIME_AXES, "freq", None), P(), P(), P(), P(), P(TIME_AXES, "freq", None))
    out_specs = (
        P(TIME_AXES, "freq", None),
        P(TIME_AXES, "freq", None),
        P(("tz", "core", "freq"), None, None),
    )
    return jax.shard_map(local, mesh=inner, in_specs=in_specs, out_specs=out_specs, check_vma=False)
```

```python
import math

import jax
import jax.numpy as jnp
from jax import lax
from jax.sharding import Mesh, PartitionSpec as P

HEADS = 8
TIME_AXES = ("tz", "core")


window_reach = 6
tile_edge = 8
span_edge = 20
norm_eps = 1e-05
far_value = -1e30


def extended(array, sides, width):
    for axis, dim in sides:
        size, length = (lax.axis_size(axis), array.shape[dim])
        up = [(i, (i + 1) % size) for i in range(size - 1)]
        down = [(j, i) for i, j in up]
        last = lax.slice_in_dim(array, length - width, length, axis=dim)
        leading = lax.slice_in_dim(array, 0, width, axis=dim)
        before = lax.ppermute(last, axis, up)
        after = lax.ppermute(leading, axis, down)
        array = jnp.concatenate([before, array, after], axis=dim)
    return array


def mix(form, left_operand, right_operand):
    return jnp.einsum(form, left_operand, right_operand, preferred_element_type=jnp.float32)


def window_mask():
    query_pos = jnp.arange(tile_edge * tile_edge)
    key_pos = jnp.arange(span_edge * span_edge)
    rise_rows = (key_pos // span_edge)[None, :] - (query_pos // tile_edge)[:, None]
    rise_cols = (key_pos % span_edge)[None, :] - (query_pos % tile_edge)[:, None]
    return (
        (rise_rows >= 0)
        & (rise_rows <= 2 * window_reach)
        & (rise_cols >= 0)
        & (rise_cols <= 2 * window_reach)
    )


def pack_tiles(field_map):
    lead, row_total, col_total = field_map.shape[:3]
    trailing = field_map.shape[3:]
    shaped = field_map.reshape(
        (lead, row_total // tile_edge, tile_edge, col_total // tile_edge, tile_edge) + trailing
    )
    axes_order = (0, 1, 3, 2, 4) + tuple(range(5, shaped.ndim))
    return shaped.transpose(axes_order).reshape(
        (lead, row_total // tile_edge * (col_total // tile_edge), tile_edge * tile_edge)
        + trailing
    )


def unpack_tiles(tile_stack, row_total, col_total):
    lead = tile_stack.shape[0]
    trailing = tile_stack.shape[3:]
    shaped = tile_stack.reshape(
        (lead, row_total // tile_edge, col_total // tile_edge, tile_edge, tile_edge) + trailing
    )
    axes_order = (0, 1, 3, 2, 4) + tuple(range(5, shaped.ndim))
    return shaped.transpose(axes_order).reshape((lead, row_total, col_total) + trailing)


def spread_tiles(field_map, row_total, col_total):
    lead = field_map.shape[0]
    trailing = field_map.shape[3:]
    spans = []
    for tile_row in range(row_total // tile_edge):
        for tile_col in range(col_total // tile_edge):
            row_at, col_at = tile_row * tile_edge, tile_col * tile_edge
            spans.append(
                field_map[:, row_at : row_at + span_edge, col_at : col_at + span_edge].reshape(
                    (lead, span_edge * span_edge) + trailing
                )
            )
    return jnp.stack(spans, axis=1)


def attend_both(q_heads, k_rim, v_rim, g_heads, key_ok, head_count):
    head_count, row_total, col_total, head_dim = q_heads.shape
    score_scale = 1.0 / math.sqrt(head_dim)
    inside = window_mask()
    q_part = pack_tiles(q_heads)
    g_part = pack_tiles(g_heads)
    k_part = spread_tiles(k_rim, row_total, col_total)
    v_part = spread_tiles(v_rim, row_total, col_total)
    ok_part = spread_tiles(key_ok[None], row_total, col_total)[0]
    allowed = inside[None, None] & (ok_part[None, :, None, :] > 0.5)
    scores = mix("hnqd,hnkd->hnqk", q_part, k_part) * score_scale
    scores = jnp.where(allowed, scores, far_value)
    row_max = jnp.max(scores, axis=-1, keepdims=True)
    log_total = row_max + jnp.log(jnp.sum(jnp.exp(scores - row_max), axis=-1, keepdims=True))
    soft_weights = jnp.where(allowed, jnp.exp(scores - log_total), 0.0)
    attended = mix("hnqk,hnkd->hnqd", soft_weights.astype(jnp.bfloat16), v_part)
    grad_probs = mix("hnqd,hnkd->hnqk", g_part, v_part)
    spread = jnp.sum(soft_weights * grad_probs, axis=-1, keepdims=True)
    grad_scores = (soft_weights * (grad_probs - spread) * score_scale).astype(jnp.bfloat16)
    grad_query = mix("hnqk,hnkd->hnqd", grad_scores, k_part)
    return (
        unpack_tiles(attended.astype(jnp.bfloat16), row_total, col_total),
        unpack_tiles(grad_query.astype(jnp.bfloat16), row_total, col_total),
        unpack_tiles(log_total[..., 0], row_total, col_total),
        unpack_tiles(spread[..., 0], row_total, col_total),
    )


def attend_key_grad(k_heads, v_heads, q_rim, g_rim, log_rim, spread_rim, head_count):
    head_count, row_total, col_total, head_dim = k_heads.shape
    score_scale = 1.0 / math.sqrt(head_dim)
    inside = window_mask()
    k_part = pack_tiles(k_heads)
    v_part = pack_tiles(v_heads)
    q_part = spread_tiles(q_rim, row_total, col_total)
    g_part = spread_tiles(g_rim, row_total, col_total)
    l_part = spread_tiles(log_rim, row_total, col_total)
    s_part = spread_tiles(spread_rim, row_total, col_total)
    scores = mix("hnkd,hnqd->hnkq", k_part, q_part) * score_scale
    soft_weights = jnp.where(inside[None, None], jnp.exp(scores - l_part[:, :, None, :]), 0.0)
    grad_probs = mix("hnkd,hnqd->hnkq", v_part, g_part)
    grad_scores = (soft_weights * (grad_probs - s_part[:, :, None, :]) * score_scale).astype(
        jnp.bfloat16
    )
    grad_keys = mix("hnkq,hnqd->hnkd", grad_scores, q_part)
    grad_values = mix("hnkq,hnqd->hnkd", soft_weights.astype(jnp.bfloat16), g_part)
    grad_pair = jnp.concatenate([grad_keys, grad_values]).astype(jnp.bfloat16)
    grad_pair = unpack_tiles(grad_pair, row_total, col_total)
    return grad_pair.reshape((2, head_count) + grad_pair.shape[1:])


def layer_norm(flat_rows):
    wide_values = flat_rows.astype(jnp.float32)
    center = jnp.mean(wide_values, axis=-1, keepdims=True)
    shifted = wide_values - center
    inverse = lax.rsqrt(jnp.mean(shifted * shifted, axis=-1, keepdims=True) + norm_eps)
    return (shifted * inverse, inverse)


def local(tokens, w_query, w_key, w_value, w_out, d_out):
    tile_rows, tile_cols, model_width = tokens.shape
    head_dim = model_width // HEADS
    token_count = tile_rows * tile_cols
    flat_rows = tokens.reshape(token_count, model_width)
    normed, inverse = layer_norm(flat_rows)
    hidden = normed.astype(jnp.bfloat16)

    def split_heads(weight):
        return weight.reshape(model_width, HEADS, head_dim)

    def project(weight):
        rows = mix("td,dhe->hte", hidden, split_heads(weight)).astype(jnp.bfloat16)
        return rows.reshape(HEADS, tile_rows, tile_cols, head_dim)

    q_heads = project(w_query)
    k_heads = project(w_key)
    v_heads = project(w_value)
    grad_flat = d_out.reshape(token_count, model_width)
    out_heads = w_out.reshape(HEADS, head_dim, model_width)
    g_heads = mix("tf,hef->hte", grad_flat, out_heads).astype(jnp.bfloat16)
    g_heads = g_heads.reshape(HEADS, tile_rows, tile_cols, head_dim)
    time_all = tile_rows * lax.axis_size(TIME_AXES)
    freq_all = tile_cols * lax.axis_size("freq")
    time_start = lax.axis_index(TIME_AXES) * tile_rows
    freq_start = lax.axis_index("freq") * tile_cols

    def inside_map(margin):
        time_pos = time_start - margin + jnp.arange(tile_rows + 2 * margin)
        freq_pos = freq_start - margin + jnp.arange(tile_cols + 2 * margin)
        time_ok = (time_pos >= 0) & (time_pos < time_all)
        freq_ok = (freq_pos >= 0) & (freq_pos < freq_all)
        return (time_ok[:, None] & freq_ok[None, :]).astype(jnp.float32)

    sides = ((TIME_AXES, 2), ("freq", 3))
    near_rim = extended(jnp.stack([k_heads, v_heads]), sides, window_reach)
    beside_all = extended(jnp.stack([q_heads, g_heads]), sides, window_reach)
    attended, grad_query, log_own, spread_own = attend_both(
        q_heads, near_rim[0], near_rim[1], g_heads, inside_map(window_reach), HEADS
    )
    stats_rim = extended(jnp.stack([log_own, spread_own]), sides, window_reach)
    grad_pair = attend_key_grad(
        k_heads, v_heads, beside_all[0], beside_all[1], stats_rim[0], stats_rim[1], HEADS
    ).reshape(2, HEADS, token_count, head_dim)
    grad_keys, grad_values = grad_pair[0], grad_pair[1]
    attended = attended.reshape(HEADS, token_count, head_dim)
    grad_query = grad_query.reshape(HEADS, token_count, head_dim)
    output = (flat_rows.astype(jnp.float32) + mix("hte,hef->tf", attended, out_heads)).astype(
        jnp.bfloat16
    )

    core = lax.axis_index("core")
    pair = [(0, 1), (1, 0)]
    hidden_split = hidden.reshape(token_count, HEADS, 2, head_dim // 2)
    attended_split = attended.reshape(HEADS, token_count, 2, head_dim // 2)
    hidden_mine = lax.dynamic_index_in_dim(hidden_split, core, axis=2, keepdims=False)
    hidden_theirs = lax.dynamic_index_in_dim(hidden_split, 1 - core, axis=2, keepdims=False)
    attended_mine = lax.dynamic_index_in_dim(attended_split, core, axis=2, keepdims=False)
    attended_theirs = lax.dynamic_index_in_dim(attended_split, 1 - core, axis=2, keepdims=False)
    hidden_got, attended_got, query_got, grad_got = lax.ppermute(
        (hidden_theirs, attended_theirs, grad_query, grad_flat), "core", pair
    )
    pair_got = lax.ppermute(grad_pair, "core", pair)
    keys_got, values_got = pair_got[0], pair_got[1]
    hidden_both = jnp.concatenate([hidden_mine, hidden_got], axis=0)
    attended_both = jnp.concatenate([attended_mine, attended_got], axis=1)
    grad_both = jnp.concatenate([grad_flat, grad_got], axis=0)
    half_rows = model_width // 2

    def weight_term(grad_heads, grad_heads_got):
        both = jnp.concatenate([grad_heads, grad_heads_got], axis=1)
        return mix("tab,hte->abhe", hidden_both, both).reshape(half_rows, model_width)

    term_rows = jnp.concatenate(
        [
            weight_term(grad_query, query_got),
            weight_term(grad_keys, keys_got),
            weight_term(grad_values, values_got),
            mix("atb,tf->abf", attended_both, grad_both).reshape(half_rows, model_width),
        ],
        axis=1,
    )
    summed = lax.psum(term_rows, ("tz", "freq"))
    row_count = model_width // (lax.axis_size(TIME_AXES) * lax.axis_size("freq"))
    row_start = (lax.axis_index("tz") * lax.axis_size("freq") + lax.axis_index("freq")) * row_count
    weight_grads = lax.dynamic_slice_in_dim(summed, row_start, row_count, axis=0).reshape(
        row_count, 4, model_width
    )
    grad_hidden = mix("hte,dhe->td", grad_query, split_heads(w_query))
    grad_hidden = grad_hidden + mix("hte,dhe->td", grad_keys, split_heads(w_key))
    grad_hidden = grad_hidden + mix("hte,dhe->td", grad_values, split_heads(w_value))
    center_grad = jnp.mean(grad_hidden, axis=-1, keepdims=True)
    along = jnp.mean(grad_hidden * normed, axis=-1, keepdims=True)
    input_grad = (
        grad_flat.astype(jnp.float32) + (grad_hidden - center_grad - normed * along) * inverse
    ).astype(jnp.bfloat16)
    return (
        output.reshape(tile_rows, tile_cols, model_width),
        input_grad.reshape(tile_rows, tile_cols, model_width),
        weight_grads,
    )


def solution(mesh):
    time_size, freq_size = mesh.shape["tm"], mesh.shape["freq"]
    inner = Mesh(mesh.devices.reshape(time_size // 2, 2, freq_size), ("tz", "core", "freq"))
    in_specs = (P(TIME_AXES, "freq", None), P(), P(), P(), P(), P(TIME_AXES, "freq", None))
    out_specs = (
        P(TIME_AXES, "freq", None),
        P(TIME_AXES, "freq", None),
        P(("tz", "core", "freq"), None, None),
    )
    return jax.shard_map(local, mesh=inner, in_specs=in_specs, out_specs=out_specs, check_vma=False)
```
